128 devices in a mesh: gx: 16 (over x_hi, z, core), gy: 8 (over x_lo, y).
Axes of the slice: x: 4 (x_hi: 2, x_lo: 2; x = x_hi * 2 + x_lo), y: 4, z: 4, core: 2. Of those that a mesh axis runs over, the one named last changes fastest.
Arguments:
- wavefunctions: float32 [192, 36864], P('gx', 'gy'), may hold values from -6 to 6
- potential: float32 [192, 576], P('gx', 'gy'), may hold values from -1 to 1
- cell_matrix: float32 [343, 343], replicated, may hold values from -0.08639188 to 1.4863919, as said below
- pair_cell: int32 [128, 256], P(('gx', 'gy')), may hold values from 0 to 3, as said below
- pair_tile: float32 [128, 256, 18, 343], P(('gx', 'gy')), may hold values from -0.2159797 to 0.2159797, as said below
- slot_atom: int32 [128, 256], P(('gx', 'gy')), may hold values from 0 to 63, as said below
- coupling: float32 [8192, 18, 18], P(('gx', 'gy')), may hold values from -0.28 to 0.28, as said below
- bounds: float32 [2, 3], replicated, may hold values from -2.5 to 15, as said below
Outputs:
- filtered: float32 [192, 36864], P('gx', 'gy')
The draws below stay inside these ranges and needn't reach their ends.
Inputs may be any that keep to these rules, and one draw needn't show every extreme that they name: `pair_cell`: slots d * 2 to d * 2 + 1 of a device go to owner d; each slot is live or padded, and a padded slot has cell 0. Some owner receives 2 live slots from every device in every draw. `slot_atom`: entry [d, s * 2 + k] names the atom on owner d of slot d * 2 + k of device s; padded slots name 0. `pair_tile`: padded slots hold all-zero tiles. `coupling`: each matrix is symmetric. `cell_matrix`: Symmetric. `bounds`: each row rises: lowest estimate, then lower end, then upper end.
All inputs are finite; a program needn't handle non-finite values.
Results may differ from the reference program's by a relative error of at most 0.0001.
Values sent between devices are 32-bit elements; how exact they have to be, the bound alone decides.
No kernel may reach another device: no remote copies, remote signals or barrier semaphores. Data moves between devices by JAX's collectives and lax.ppermute only.
A program may use at most 128 MiB of HBM per device.

```python
import jax
import jax.numpy as jnp
from jax import lax

DEG = 6
NPC = 343
W = 64
NPROJ = 18
CX = 2
CY = 1
CZ = 2
ATOM_DEV = 64
CAP = 2
ORDER = 2
FILTERS = 2
OWNERS = 128
SLOTS = 256
ZN = 12
NXN = 192
NYN = 48
N_GX = 16
N_GY = 8


def live_slots(key):
    base = jax.random.fold_in(key, 7)
    key_counts, key_busy, key_full = jax.random.split(base, 3)
    counts = jax.random.randint(key_counts, (OWNERS, OWNERS), 0, CAP + 1)
    busy_owner = (jax.random.randint(key_busy, (1, OWNERS), 0, 4) == 0).astype(jnp.int32)
    counts = jnp.minimum(counts + busy_owner, CAP)
    full_owner = jax.random.randint(key_full, (), 0, OWNERS)
    counts = jnp.where(jnp.arange(OWNERS)[None, :] == full_owner, CAP, counts)
    return jnp.arange(CAP)[None, None, :] < counts[:, :, None]


def rough_values(key, shape):
    return jnp.clip(jax.random.normal(key, shape, jnp.float32), -4.0, 4.0)


def draw_pair_cell(key, part):
    live = live_slots(key).reshape(OWNERS, SLOTS)
    cell_ids = jax.random.randint(jax.random.fold_in(key, 17), (OWNERS, SLOTS), 0, CX * CY * CZ)
    return jnp.where(live, cell_ids, 0).astype(jnp.int32)


def draw_slot_atom(key, part):
    live = live_slots(key).transpose(1, 0, 2).reshape(OWNERS, SLOTS)
    atom_ids = jax.random.randint(jax.random.fold_in(key, 27), (OWNERS, SLOTS), 0, ATOM_DEV)
    return jnp.where(live, atom_ids, 0).astype(jnp.int32)


def draw_pair_tile(key, part):
    live = live_slots(key).reshape(OWNERS, SLOTS, 1, 1).astype(jnp.float32)
    values = rough_values(jax.random.fold_in(key, 37), (OWNERS, SLOTS, NPROJ, NPC))
    return values * live * (1.0 / NPC ** 0.5)


def draw_coupling(key, part):
    values = rough_values(jax.random.fold_in(key, 47), (OWNERS * ATOM_DEV, NPROJ, NPROJ))
    return (values + jnp.swapaxes(values, 1, 2)) * 0.035


def draw_cell_matrix(key, part):
    values = rough_values(jax.random.fold_in(key, 57), (NPC, NPC))
    diagonal = jax.random.uniform(jax.random.fold_in(key, 67), (NPC,), jnp.float32, 0.6, 1.4)
    return (values + values.T) * (0.2 / NPC ** 0.5) + jnp.diag(diagonal)


def draw_bounds(key, part):
    lowest = jax.random.uniform(jax.random.fold_in(key, 71), (FILTERS,), jnp.float32, -2.5, -1.5)
    lower_end = jax.random.uniform(jax.random.fold_in(key, 73), (FILTERS,), jnp.float32, 1.5, 2.5)
    upper_end = jax.random.uniform(jax.random.fold_in(key, 79), (FILTERS,), jnp.float32, 13.0, 15.0)
    return jnp.stack([lowest, lower_end, upper_end], axis=1)


def shard_levels(rng, dims, shards, least, high):
    def one(dim, shards_of):
        draws = jax.random.uniform(jax.random.fold_in(jax.random.fold_in(rng, 6), dim), (shards_of,), jnp.float32, least / len(shards), high / len(shards))
        return jnp.repeat(jnp.exp(draws), dims[dim] // shards_of).reshape((-1,) + (1,) * (len(dims) - dim - 1))

    gain = one(*shards[0])
    for cut in shards[1:]:
        gain = gain * one(*cut)
    return gain


def centred(rng, extent, scale, limit, shards=(), kind=jnp.bfloat16):
    values = scale * jax.random.normal(rng, extent, jnp.float32)
    if shards:
        values = values * shard_levels(rng, extent, shards, -0.22, 0.18)
    return jnp.clip(values, -limit, limit).astype(kind)


def setup_inputs(seed: int = 0) -> dict:
    key_list = jax.random.split(jax.random.key(seed), 9)
    return {
        "wavefunctions": centred(key_list[0], (NXN, NYN * ZN * W), 1.0, 6.0, ((0, 16), (1, 8)), jnp.float32),
        "potential": jnp.clip(jax.random.uniform(key_list[1], (NXN, NYN * ZN), jnp.float32, -1.0, 1.0) * shard_levels(key_list[1], (NXN, NYN * ZN), ((0, 16), (1, 8)), -0.4, 0.0), -1.0, 1.0),
        "cell_matrix": draw_cell_matrix(jax.random.fold_in(key_list[8], 71), 0),
        "pair_cell": draw_pair_cell(jax.random.fold_in(key_list[8], 71), 0),
        "pair_tile": draw_pair_tile(jax.random.fold_in(key_list[8], 71), 0),
        "slot_atom": draw_slot_atom(jax.random.fold_in(key_list[8], 71), 0),
        "coupling": draw_coupling(jax.random.fold_in(key_list[8], 71), 0),
        "bounds": draw_bounds(jax.random.fold_in(key_list[8], 71), 0),
    }


PRECISE = lax.Precision.HIGHEST


def split_lead(values, number):
    trailing = values.shape[1:]
    leading_part = values[: number * DEG].reshape((number, DEG) + trailing)
    upper_part = values[DEG::DEG][:, None]
    return jnp.concatenate([leading_part, upper_part], axis=1)


def join_lead(values):
    number = values.shape[0]
    trailing = values.shape[2:]
    leading_part = values[:, :DEG].reshape((number * DEG,) + trailing)
    leading_part = jnp.concatenate([leading_part, jnp.zeros((1,) + trailing, jnp.float32)], axis=0)
    upper_part = jnp.zeros((number + 1, DEG) + trailing, jnp.float32).at[1:, 0].set(values[:, DEG])
    upper_part = upper_part.reshape(((number + 1) * DEG,) + trailing)[: number * DEG + 1]
    return leading_part + upper_part


def gather_cells(extended, cells_x, cells_y, cells_z):
    closed = jnp.concatenate([extended, extended[:, :, :1]], axis=2)
    layered = split_lead(closed, cells_x)
    layered = split_lead(jnp.moveaxis(layered, 2, 0), cells_y)
    layered = split_lead(jnp.moveaxis(layered, 4, 0), cells_z)
    layered = layered.transpose(5, 3, 1, 4, 2, 0, 6)
    return layered.reshape((DEG + 1) ** 3, cells_x * cells_y * cells_z, layered.shape[-1])


def scatter_cells(cell_out, cells_x, cells_y, cells_z):
    columns = cell_out.shape[-1]
    layered = cell_out.reshape(DEG + 1, DEG + 1, DEG + 1, cells_x, cells_y, cells_z, columns)
    layered = layered.transpose(5, 2, 4, 1, 3, 0, 6)
    layered = join_lead(layered)
    layered = layered[:-1].at[0].add(layered[-1])
    layered = join_lead(jnp.moveaxis(layered, 0, 4))
    layered = join_lead(jnp.moveaxis(layered, 0, 3))
    return layered.transpose(0, 2, 1, 3)


def apply_operator(current, node_potential, cell_matrix, pair_cell, pair_tile, slot_atom, coupling):
    cells_x = NXN // DEG
    cells_y = NYN // DEG
    extended = jnp.concatenate([current, current[:1]], axis=0)
    extended = jnp.concatenate([extended, extended[:, :1]], axis=1)
    cell_in = gather_cells(extended, cells_x, cells_y, CZ)
    kinetic = jnp.dot(cell_matrix, cell_in.reshape(NPC, -1), precision=PRECISE).reshape(cell_in.shape)
    by_device = cell_in.reshape(NPC, N_GX, CX, N_GY, CY, CZ, W).transpose(1, 3, 0, 2, 4, 5, 6)
    by_device = by_device.reshape(OWNERS, NPC, CX * CY * CZ, W)

    def project(members):
        device_cells, cell_ids, tile_set = members
        picked = jnp.take(device_cells, cell_ids, axis=1)
        return jnp.einsum("spn,nsw->spw", tile_set, picked, precision=PRECISE)

    projected = lax.map(project, (by_device, pair_cell, pair_tile))
    at_owner = projected.reshape(OWNERS, OWNERS, CAP, NPROJ, W).transpose(1, 0, 2, 3, 4)
    at_owner = at_owner.reshape(OWNERS, SLOTS, NPROJ, W)
    one_hot = (slot_atom[:, :, None] == jnp.arange(ATOM_DEV, dtype=jnp.int32)[None, None, :]).astype(jnp.float32)
    atom_sums = jnp.einsum("dsa,dspw->dapw", one_hot, at_owner, precision=PRECISE)
    applied = jnp.einsum("dapq,daqw->dapw", coupling.reshape(OWNERS, ATOM_DEV, NPROJ, NPROJ), atom_sums, precision=PRECISE)
    answers = jnp.einsum("dsa,dapw->dspw", one_hot, applied, precision=PRECISE)
    returned = answers.reshape(OWNERS, OWNERS, CAP, NPROJ, W).transpose(1, 0, 2, 3, 4)
    returned = returned.reshape(OWNERS, SLOTS, NPROJ, W)

    def deposit(members):
        cell_ids, tile_set, coeffs = members
        spread = jnp.einsum("spn,spw->nsw", tile_set, coeffs, precision=PRECISE)
        return jnp.zeros((NPC, CX * CY * CZ, W), jnp.float32).at[:, cell_ids].add(spread)

    deposits = lax.map(deposit, (pair_cell, pair_tile, returned))
    projector_part = deposits.reshape(N_GX, N_GY, NPC, CX, CY, CZ, W).transpose(2, 0, 3, 1, 4, 5, 6)
    projector_part = projector_part.reshape(NPC, cells_x * cells_y * CZ, W)
    summed = scatter_cells(kinetic + projector_part, cells_x, cells_y, CZ)
    summed = summed[:, :-1].at[:, 0].add(summed[:, -1])
    summed = summed[:-1].at[0].add(summed[-1])
    return summed + node_potential * current


def reference(wavefunctions, potential, cell_matrix, pair_cell, pair_tile, slot_atom, coupling, bounds):
    node_potential = potential.reshape(NXN, NYN, ZN, 1)
    previous = wavefunctions.reshape(NXN, NYN, ZN, W)

    def operator(field):
        return apply_operator(field, node_potential, cell_matrix, pair_cell, pair_tile, slot_atom, coupling)

    for filter_index in range(FILTERS):
        lower_bound = bounds[filter_index, 0]
        low_end = bounds[filter_index, 1]
        high_end = bounds[filter_index, 2]
        half_width = (high_end - low_end) / 2.0
        centre = (high_end + low_end) / 2.0
        sigma_now = half_width / (lower_bound - centre)
        gamma_term = 2.0 / sigma_now
        current = (sigma_now / half_width) * (operator(previous) - centre * previous)
        for repeat in range(ORDER - 1):
            sigma_next = 1.0 / (gamma_term - sigma_now)
            following = (2.0 * sigma_next / half_width) * (operator(current) - centre * current) - (sigma_now * sigma_next) * previous
            previous = current
            current = following
            sigma_now = sigma_next
        previous = current
    return previous.reshape(NXN, NYN * ZN * W)
```

```python
import jax
import jax.numpy as jnp
from jax import lax
from jax.sharding import PartitionSpec as P

DEG = 6
W = 64
CX = 2
CY = 1
CZ = 2
FILTERS = 2
ZN = 12


PRECISE = lax.Precision.HIGHEST


def shifted(value, axis, steps):
    count = lax.axis_size(axis)
    pairs = [(source, (source + steps) % count) for source in range(count)]
    return lax.ppermute(value, axis, pairs)


def cell_ranges():
    for p in range(CX):
        for q in range(CY):
            for r in range(CZ):
                yield p * DEG, q * DEG, r * DEG


def gather_cells(extended):
    closed = jnp.concatenate([extended, extended[:, :, :1]], axis=2)
    blocks = [
        closed[x0 : x0 + DEG + 1, y0 : y0 + DEG + 1, z0 : z0 + DEG + 1]
        for x0, y0, z0 in cell_ranges()
    ]
    stacked = jnp.stack(blocks, axis=3)
    return stacked.reshape((DEG + 1) ** 3, len(blocks) * stacked.shape[-1])


def scatter_cells(cell_out, columns):
    cells = cell_out.shape[1] // columns
    blocks = cell_out.reshape(DEG + 1, DEG + 1, DEG + 1, cells, columns)
    nx, ny, nz = CX * DEG + 1, CY * DEG + 1, CZ * DEG + 1
    total = None
    for index, (x0, y0, z0) in enumerate(cell_ranges()):
        padded = jnp.pad(
            blocks[:, :, :, index],
            ((x0, nx - x0 - DEG - 1), (y0, ny - y0 - DEG - 1), (z0, nz - z0 - DEG - 1), (0, 0)),
        )
        total = padded if total is None else total + padded
    return total[:, :, :ZN].at[:, :, 0].add(total[:, :, ZN])


def body(wavefunctions, potential, cell_matrix, pair_cell, pair_tile, slot_atom, coupling, bounds):
    rows_x = wavefunctions.shape[0]
    rows_y = potential.shape[1] // ZN
    slots, nproj, npc = pair_tile.shape[1:]
    atoms = coupling.shape[0]
    cells = CX * CY * CZ
    owners = lax.axis_size(("gx", "gy"))
    local_pot = potential.reshape(rows_x, rows_y, ZN, 1)
    tile_flat = pair_tile[0].reshape(slots * nproj, npc)
    cell_mask = (pair_cell[0][:, None] == jnp.arange(cells, dtype=jnp.int32)[None, :]).astype(jnp.float32)
    row_mask = jnp.repeat(cell_mask, nproj, axis=0)[:, :, None]
    one_hot = (
        slot_atom[0][:, None] == jnp.arange(atoms, dtype=jnp.int32)[None, :]
    ).astype(jnp.float32)

    def exchange(values):
        return lax.all_to_all(values, ("gx", "gy"), split_axis=0, concat_axis=0, tiled=True)

    def owner_work(received):
        atom_sums = lax.dot_general(
            one_hot, received, (((0,), (0,)), ((), ())), precision=PRECISE
        ).reshape(atoms, nproj, W)
        applied = jnp.einsum("apq,aqw->apw", coupling, atom_sums, precision=PRECISE)
        return jnp.dot(one_hot, applied.reshape(atoms, nproj * W), precision=PRECISE)

    def apply_operator(current):
        face_in = shifted(current[:1], "gx", -1)
        extended = jnp.concatenate([current, face_in], axis=0)
        side_in = shifted(extended[:, :1], "gy", -1)
        extended = jnp.concatenate([extended, side_in], axis=1)
        cell_in = gather_cells(extended)
        every_cell = jnp.dot(tile_flat, cell_in, precision=PRECISE)
        projected = (every_cell.reshape(slots * nproj, cells, W) * row_mask).sum(axis=1)
        received = exchange(projected.reshape(owners, -1)).reshape(slots, nproj * W)
        returned = exchange(owner_work(received).reshape(owners, -1))
        spread_in = (returned.reshape(slots * nproj, 1, W) * row_mask).reshape(slots * nproj, cells * W)
        kinetic = jnp.dot(cell_matrix, cell_in, precision=PRECISE)
        spread = lax.dot_general(
            tile_flat, spread_in, (((0,), (0,)), ((), ())), precision=PRECISE
        )
        summed = scatter_cells(kinetic + spread, W)
        arrived = shifted(summed[:, rows_y], "gy", 1)
        summed = summed[:, :rows_y].at[:, 0].add(arrived)
        arrived_x = shifted(summed[rows_x], "gx", 1)
        summed = summed[:rows_x].at[0].add(arrived_x)
        return summed + local_pot * current

    previous = wavefunctions.reshape(rows_x, rows_y, ZN, W)
    for filter_index in range(FILTERS):
        lower_bound = bounds[filter_index, 0]
        low_end = bounds[filter_index, 1]
        high_end = bounds[filter_index, 2]
        half_width = (high_end - low_end) / 2.0
        centre = (high_end + low_end) / 2.0
        sigma_now = half_width / (lower_bound - centre)
        gamma_term = 2.0 / sigma_now
        current = sigma_now / half_width * (apply_operator(previous) - centre * previous)
        sigma_next = 1.0 / (gamma_term - sigma_now)
        following = (
            2.0 * sigma_next / half_width * (apply_operator(current) - centre * current)
            - sigma_now * sigma_next * previous
        )
        current = following
        sigma_now = sigma_next
        previous = current
    return previous.reshape(rows_x, rows_y * ZN * W)


def solution(mesh):
    placed = (
        P("gx", "gy"),
        P("gx", "gy"),
        P(),
        P(("gx", "gy"), None),
        P(("gx", "gy"), None, None, None),
        P(("gx", "gy"), None),
        P(("gx", "gy"), None, None),
        P(),
    )
    return jax.shard_map(body, mesh=mesh, in_specs=placed, out_specs=P("gx", "gy"), check_vma=False)
```

```python
import jax
import jax.numpy as jnp
from jax import lax
from jax.sharding import PartitionSpec as P

DEG = 6
W = 64
CX = 2
CY = 1
CZ = 2
FILTERS = 2
ZN = 12


PRECISE = lax.Precision.HIGHEST
DENSE = lax.Precision.HIGH


def shifted(value, axis, steps):
    count = lax.axis_size(axis)
    pairs = [(source, (source + steps) % count) for source in range(count)]
    return lax.ppermute(value, axis, pairs)


def diagonal(value, steps):
    count_x = lax.axis_size("gx")
    count_y = lax.axis_size("gy")
    pairs = [
        (u * count_y + v, ((u + steps) % count_x) * count_y + (v + steps) % count_y)
        for u in range(count_x)
        for v in range(count_y)
    ]
    return lax.ppermute(value, ("gx", "gy"), pairs)


def cell_ranges():
    for p in range(CX):
        for q in range(CY):
            for r in range(CZ):
                yield p * DEG, q * DEG, r * DEG


def gather_cells(extended):
    closed = jnp.concatenate([extended, extended[:, :, :1]], axis=2)
    blocks = [
        closed[x0 : x0 + DEG + 1, y0 : y0 + DEG + 1, z0 : z0 + DEG + 1]
        for x0, y0, z0 in cell_ranges()
    ]
    stacked = jnp.stack(blocks, axis=3)
    return stacked.reshape((DEG + 1) ** 3, len(blocks) * stacked.shape[-1])


def scatter_cells(cell_out, columns):
    cells = cell_out.shape[1] // columns
    blocks = cell_out.reshape(DEG + 1, DEG + 1, DEG + 1, cells, columns)
    nx, ny, nz = CX * DEG + 1, CY * DEG + 1, CZ * DEG + 1
    total = None
    for index, (x0, y0, z0) in enumerate(cell_ranges()):
        padded = jnp.pad(
            blocks[:, :, :, index],
            ((x0, nx - x0 - DEG - 1), (y0, ny - y0 - DEG - 1), (z0, nz - z0 - DEG - 1), (0, 0)),
        )
        total = padded if total is None else total + padded
    return total[:, :, :ZN].at[:, :, 0].add(total[:, :, ZN])


def body(wavefunctions, potential, cell_matrix, pair_cell, pair_tile, slot_atom, coupling, bounds):
    rows_x = wavefunctions.shape[0]
    rows_y = potential.shape[1] // ZN
    slots, nproj, npc = pair_tile.shape[1:]
    atoms = coupling.shape[0]
    cells = CX * CY * CZ
    owners = lax.axis_size(("gx", "gy"))
    local_pot = potential.reshape(rows_x, rows_y, ZN, 1)
    tile_flat = pair_tile[0].reshape(slots * nproj, npc)
    cell_mask = (pair_cell[0][:, None] == jnp.arange(cells, dtype=jnp.int32)[None, :]).astype(jnp.float32)
    row_mask = jnp.repeat(cell_mask, nproj, axis=0)[:, :, None]
    one_hot = (
        slot_atom[0][:, None] == jnp.arange(atoms, dtype=jnp.int32)[None, :]
    ).astype(jnp.float32)

    def exchange(values):
        return lax.all_to_all(values, ("gx", "gy"), split_axis=0, concat_axis=0, tiled=True)

    def owner_work(received):
        atom_sums = lax.dot_general(
            one_hot, received, (((0,), (0,)), ((), ())), precision=PRECISE
        ).reshape(atoms, nproj, W)
        applied = jnp.einsum("apq,aqw->apw", coupling, atom_sums, precision=PRECISE)
        return jnp.dot(one_hot, applied.reshape(atoms, nproj * W), precision=PRECISE)

    def apply_operator(current):
        face_x = shifted(current[:1], "gx", -1)
        face_y = shifted(current[:, :1], "gy", -1)
        corner = diagonal(current[:1, :1], -1)
        extended = jnp.concatenate(
            [
                jnp.concatenate([current, face_y], axis=1),
                jnp.concatenate([face_x, corner], axis=1),
            ],
            axis=0,
        )
        cell_in = gather_cells(extended)
        every_cell = jnp.dot(tile_flat, cell_in, precision=DENSE)
        projected = (every_cell.reshape(slots * nproj, cells, W) * row_mask).sum(axis=1)
        received = exchange(projected.reshape(owners, -1)).reshape(slots, nproj * W)
        returned = exchange(owner_work(received).reshape(owners, -1))
        spread_in = (returned.reshape(slots * nproj, 1, W) * row_mask).reshape(slots * nproj, cells * W)
        kinetic = jnp.dot(cell_matrix, cell_in, precision=DENSE)
        spread = lax.dot_general(
            tile_flat, spread_in, (((0,), (0,)), ((), ())), precision=DENSE
        )
        summed = scatter_cells(kinetic + spread, W)
        from_y = shifted(summed[:rows_x, rows_y], "gy", 1)
        from_x = shifted(summed[rows_x, :rows_y], "gx", 1)
        from_corner = diagonal(summed[rows_x, rows_y], 1)
        summed = summed[:rows_x, :rows_y].at[:, 0].add(from_y)
        summed = summed.at[0].add(from_x).at[0, 0].add(from_corner)
        return summed + local_pot * current

    previous = wavefunctions.reshape(rows_x, rows_y, ZN, W)
    for filter_index in range(FILTERS):
        lower_bound = bounds[filter_index, 0]
        low_end = bounds[filter_index, 1]
        high_end = bounds[filter_index, 2]
        half_width = (high_end - low_end) / 2.0
        centre = (high_end + low_end) / 2.0
        sigma_now = half_width / (lower_bound - centre)
        gamma_term = 2.0 / sigma_now
        current = sigma_now / half_width * (apply_operator(previous) - centre * previous)
        sigma_next = 1.0 / (gamma_term - sigma_now)
        following = (
            2.0 * sigma_next / half_width * (apply_operator(current) - centre * current)
            - sigma_now * sigma_next * previous
        )
        current = following
        sigma_now = sigma_next
        previous = current
    return previous.reshape(rows_x, rows_y * ZN * W)


def solution(mesh):
    placed = (
        P("gx", "gy"),
        P("gx", "gy"),
        P(),
        P(("gx", "gy"), None),
        P(("gx", "gy"), None, None, None),
        P(("gx", "gy"), None),
        P(("gx", "gy"), None, None),
        P(),
    )
    return jax.shard_map(body, mesh=mesh, in_specs=placed, out_specs=P("gx", "gy"), check_vma=False)
```

```python
import jax
import jax.numpy as jnp
from jax import lax
from jax.sharding import PartitionSpec as P

DEG = 6
W = 64
CX = 2
CY = 1
CZ = 2
FILTERS = 2
ZN = 12
CAP = 2


PRECISE = lax.Precision.HIGHEST
DENSE = lax.Precision.HIGH


def shifted(value, axis, steps):
    count = lax.axis_size(axis)
    pairs = [(source, (source + steps) % count) for source in range(count)]
    return lax.ppermute(value, axis, pairs)


def diagonal(value, steps):
    count_x = lax.axis_size("gx")
    count_y = lax.axis_size("gy")
    pairs = [
        (u * count_y + v, ((u + steps) % count_x) * count_y + (v + steps) % count_y)
        for u in range(count_x)
        for v in range(count_y)
    ]
    return lax.ppermute(value, ("gx", "gy"), pairs)


def cell_ranges():
    for p in range(CX):
        for q in range(CY):
            for r in range(CZ):
                yield p * DEG, q * DEG, r * DEG


def gather_cells(extended):
    closed = jnp.concatenate([extended, extended[:, :, :1]], axis=2)
    blocks = [
        closed[x0 : x0 + DEG + 1, y0 : y0 + DEG + 1, z0 : z0 + DEG + 1]
        for x0, y0, z0 in cell_ranges()
    ]
    stacked = jnp.stack(blocks, axis=3)
    return stacked.reshape((DEG + 1) ** 3, len(blocks) * stacked.shape[-1])


def scatter_cells(cell_out, columns):
    cells = cell_out.shape[1] // columns
    blocks = cell_out.reshape(DEG + 1, DEG + 1, DEG + 1, cells, columns)
    nx, ny, nz = CX * DEG + 1, CY * DEG + 1, CZ * DEG + 1
    total = None
    for index, (x0, y0, z0) in enumerate(cell_ranges()):
        padded = jnp.pad(
            blocks[:, :, :, index],
            ((x0, nx - x0 - DEG - 1), (y0, ny - y0 - DEG - 1), (z0, nz - z0 - DEG - 1), (0, 0)),
        )
        total = padded if total is None else total + padded
    return total[:, :, :ZN].at[:, :, 0].add(total[:, :, ZN])


def body(wavefunctions, potential, cell_matrix, pair_cell, pair_tile, slot_atom, coupling, bounds):
    rows_x = wavefunctions.shape[0]
    rows_y = potential.shape[1] // ZN
    slots, nproj, npc = pair_tile.shape[1:]
    atoms = coupling.shape[0]
    cells = CX * CY * CZ
    owners = lax.axis_size(("gx", "gy"))
    local_pot = potential.reshape(rows_x, rows_y, ZN, 1)
    cell_mask = (pair_cell[0][:, None] == jnp.arange(cells, dtype=jnp.int32)[None, :]).astype(jnp.float32)
    one_hot = (
        slot_atom[0][:, None] == jnp.arange(atoms, dtype=jnp.int32)[None, :]
    ).astype(jnp.float32)
    rows = -(-nproj // 8) * 8
    tiles = pair_tile[0].reshape(owners, CAP, nproj, npc)
    tiles = jnp.pad(tiles, ((0, 0), (0, 0), (0, rows - nproj), (0, 0)))
    tile_k = [tiles[:, k].reshape(owners * rows, npc) for k in range(CAP)]
    slot_cells = cell_mask.reshape(owners, CAP, cells)
    mask_k = [slot_cells[:, k][:, None, :, None] for k in range(CAP)]
    incoming = one_hot.reshape(owners, CAP, atoms)
    hot_k = [incoming[:, k] for k in range(CAP)]
    coupling_pad = jnp.pad(coupling, ((0, 0), (0, rows - nproj), (0, rows - nproj)))

    def exchange(values):
        return lax.all_to_all(values, ("gx", "gy"), split_axis=0, concat_axis=0, tiled=True)

    def owner_work(received):
        atom_sums = None
        for k in range(CAP):
            full = jnp.einsum("sa,spx->apx", hot_k[k], received, precision=PRECISE)
            part = full[:, :, k * W : (k + 1) * W]
            atom_sums = part if atom_sums is None else atom_sums + part
        applied = jnp.einsum("apq,aqw->apw", coupling_pad, atom_sums, precision=PRECISE)
        return jnp.concatenate(
            [jnp.einsum("sa,apw->spw", hot_k[k], applied, precision=PRECISE) for k in range(CAP)],
            axis=-1,
        )

    def apply_operator(current):
        face_x = shifted(current[:1], "gx", -1)
        face_y = shifted(current[:, :1], "gy", -1)
        corner = diagonal(current[:1, :1], -1)
        extended = jnp.concatenate(
            [
                jnp.concatenate([current, face_y], axis=1),
                jnp.concatenate([face_x, corner], axis=1),
            ],
            axis=0,
        )
        cell_in = gather_cells(extended)
        parts = []
        for k in range(CAP):
            every_cell = jnp.dot(tile_k[k], cell_in, precision=DENSE)
            parts.append((every_cell.reshape(owners, rows, cells, W) * mask_k[k]).sum(axis=2))
        returned = exchange(owner_work(exchange(jnp.concatenate(parts, axis=-1))))
        spread = jnp.dot(cell_matrix, cell_in, precision=DENSE)
        for k in range(CAP):
            part = returned[:, :, k * W : (k + 1) * W]
            spread_in = (part[:, :, None, :] * mask_k[k]).reshape(owners * rows, cells * W)
            spread = spread + lax.dot_general(
                tile_k[k], spread_in, (((0,), (0,)), ((), ())), precision=DENSE
            )
        summed = scatter_cells(spread, W)
        from_y = shifted(summed[:rows_x, rows_y], "gy", 1)
        from_x = shifted(summed[rows_x, :rows_y], "gx", 1)
        from_corner = diagonal(summed[rows_x, rows_y], 1)
        summed = summed[:rows_x, :rows_y].at[:, 0].add(from_y)
        summed = summed.at[0].add(from_x).at[0, 0].add(from_corner)
        return summed + local_pot * current

    previous = wavefunctions.reshape(rows_x, rows_y, ZN, W)
    for filter_index in range(FILTERS):
        lower_bound = bounds[filter_index, 0]
        low_end = bounds[filter_index, 1]
        high_end = bounds[filter_index, 2]
        half_width = (high_end - low_end) / 2.0
        centre = (high_end + low_end) / 2.0
        sigma_now = half_width / (lower_bound - centre)
        gamma_term = 2.0 / sigma_now
        current = sigma_now / half_width * (apply_operator(previous) - centre * previous)
        sigma_next = 1.0 / (gamma_term - sigma_now)
        following = (
            2.0 * sigma_next / half_width * (apply_operator(current) - centre * current)
            - sigma_now * sigma_next * previous
        )
        current = following
        sigma_now = sigma_next
        previous = current
    return previous.reshape(rows_x, rows_y * ZN * W)


def solution(mesh):
    placed = (
        P("gx", "gy"),
        P("gx", "gy"),
        P(),
        P(("gx", "gy"), None),
        P(("gx", "gy"), None, None, None),
        P(("gx", "gy"), None),
        P(("gx", "gy"), None, None),
        P(),
    )
    return jax.shard_map(body, mesh=mesh, in_specs=placed, out_specs=P("gx", "gy"), check_vma=False)
```

```python
import jax
import jax.numpy as jnp
from jax import lax
from jax.sharding import PartitionSpec as P

DEG = 6
W = 64
CX = 2
CY = 1
CZ = 2
FILTERS = 2
ZN = 12
CAP = 2


PRECISE = lax.Precision.HIGHEST
DENSE = lax.Precision.HIGH


def shifted(value, axis, steps):
    count = lax.axis_size(axis)
    pairs = [(source, (source + steps) % count) for source in range(count)]
    return lax.ppermute(value, axis, pairs)


def diagonal(value, steps):
    count_x = lax.axis_size("gx")
    count_y = lax.axis_size("gy")
    pairs = [
        (u * count_y + v, ((u + steps) % count_x) * count_y + (v + steps) % count_y)
        for u in range(count_x)
        for v in range(count_y)
    ]
    return lax.ppermute(value, ("gx", "gy"), pairs)


def cell_ranges():
    for p in range(CX):
        for q in range(CY):
            for r in range(CZ):
                yield p * DEG, q * DEG, r * DEG


def gather_cells(extended):
    closed = jnp.concatenate([extended, extended[:, :, :1]], axis=2)
    blocks = [
        closed[x0 : x0 + DEG + 1, y0 : y0 + DEG + 1, z0 : z0 + DEG + 1]
        for x0, y0, z0 in cell_ranges()
    ]
    stacked = jnp.stack(blocks, axis=3)
    return stacked.reshape((DEG + 1) ** 3, len(blocks) * stacked.shape[-1])


def scatter_cells(cell_out, columns):
    cells = cell_out.shape[1] // columns
    blocks = cell_out.reshape(DEG + 1, DEG + 1, DEG + 1, cells, columns)
    nx, ny, nz = CX * DEG + 1, CY * DEG + 1, CZ * DEG + 1
    total = None
    for index, (x0, y0, z0) in enumerate(cell_ranges()):
        padded = jnp.pad(
            blocks[:, :, :, index],
            ((x0, nx - x0 - DEG - 1), (y0, ny - y0 - DEG - 1), (z0, nz - z0 - DEG - 1), (0, 0)),
        )
        total = padded if total is None else total + padded
    return total[:, :, :ZN].at[:, :, 0].add(total[:, :, ZN])


def body(wavefunctions, potential, cell_matrix, pair_cell, pair_tile, slot_atom, coupling, bounds):
    rows_x = wavefunctions.shape[0]
    rows_y = potential.shape[1] // ZN
    slots, nproj, npc = pair_tile.shape[1:]
    atoms = coupling.shape[0]
    cells = CX * CY * CZ
    owners = lax.axis_size(("gx", "gy"))
    local_pot = potential.reshape(rows_x, rows_y, ZN, 1)
    cell_mask = (pair_cell[0][:, None] == jnp.arange(cells, dtype=jnp.int32)[None, :]).astype(jnp.float32)
    one_hot = (
        slot_atom[0][:, None] == jnp.arange(atoms, dtype=jnp.int32)[None, :]
    ).astype(jnp.float32)
    rows = -(-nproj // 8) * 8
    tile_set = pair_tile[0]
    tile_k = [
        jnp.pad(tile_set[k::CAP], ((0, 0), (0, rows - nproj), (0, 0))).reshape(owners * rows, npc)
        for k in range(CAP)
    ]
    tile_t = [tile.T for tile in tile_k]
    slot_cells = cell_mask.reshape(owners, CAP, cells)
    mask_k = [jnp.repeat(slot_cells[:, k], rows, axis=0) for k in range(CAP)]
    incoming = one_hot.reshape(owners, CAP, atoms)
    hot_k = [incoming[:, k] for k in range(CAP)]
    coupling_pad = jnp.pad(coupling, ((0, 0), (0, rows - nproj), (0, rows - nproj)))

    def exchange(values):
        return lax.all_to_all(values, ("gx", "gy"), split_axis=0, concat_axis=0, tiled=True)

    def owner_work(received):
        atom_sums = None
        for k in range(CAP):
            full = jnp.einsum("sa,spx->apx", hot_k[k], received, precision=PRECISE)
            part = full[:, :, k * W : (k + 1) * W]
            atom_sums = part if atom_sums is None else atom_sums + part
        applied = jnp.einsum("apq,aqw->apw", coupling_pad, atom_sums, precision=PRECISE)
        return jnp.concatenate(
            [jnp.einsum("sa,apw->spw", hot_k[k], applied, precision=PRECISE) for k in range(CAP)],
            axis=-1,
        )

    def apply_operator(current):
        face_x = shifted(current[:1], "gx", -1)
        face_y = shifted(current[:, :1], "gy", -1)
        corner = diagonal(current[:1, :1], -1)
        extended = jnp.concatenate(
            [
                jnp.concatenate([current, face_y], axis=1),
                jnp.concatenate([face_x, corner], axis=1),
            ],
            axis=0,
        )
        cell_in = gather_cells(extended)
        parts = []
        for k in range(CAP):
            every_cell = jnp.dot(tile_k[k], cell_in, precision=DENSE)
            picked = None
            for c in range(cells):
                term = every_cell[:, c * W : (c + 1) * W] * mask_k[k][:, c : c + 1]
                picked = term if picked is None else picked + term
            parts.append(picked.reshape(owners, rows, W))
        returned = exchange(owner_work(exchange(jnp.concatenate(parts, axis=-1))))
        spread = jnp.dot(cell_matrix, cell_in, precision=DENSE)
        for k in range(CAP):
            part = returned[:, :, k * W : (k + 1) * W].reshape(owners * rows, W)
            spread_in = jnp.concatenate(
                [part * mask_k[k][:, c : c + 1] for c in range(cells)], axis=1
            )
            spread = spread + jnp.dot(tile_t[k], spread_in, precision=DENSE)
        summed = scatter_cells(spread, W)
        from_y = shifted(summed[:rows_x, rows_y], "gy", 1)
        from_x = shifted(summed[rows_x, :rows_y], "gx", 1)
        from_corner = diagonal(summed[rows_x, rows_y], 1)
        summed = summed[:rows_x, :rows_y].at[:, 0].add(from_y)
        summed = summed.at[0].add(from_x).at[0, 0].add(from_corner)
        return summed + local_pot * current

    previous = wavefunctions.reshape(rows_x, rows_y, ZN, W)
    for filter_index in range(FILTERS):
        lower_bound = bounds[filter_index, 0]
        low_end = bounds[filter_index, 1]
        high_end = bounds[filter_index, 2]
        half_width = (high_end - low_end) / 2.0
        centre = (high_end + low_end) / 2.0
        sigma_now = half_width / (lower_bound - centre)
        gamma_term = 2.0 / sigma_now
        current = sigma_now / half_width * (apply_operator(previous) - centre * previous)
        sigma_next = 1.0 / (gamma_term - sigma_now)
        following = (
            2.0 * sigma_next / half_width * (apply_operator(current) - centre * current)
            - sigma_now * sigma_next * previous
        )
        current = following
        sigma_now = sigma_next
        previous = current
    return previous.reshape(rows_x, rows_y * ZN * W)


def solution(mesh):
    placed = (
        P("gx", "gy"),
        P("gx", "gy"),
        P(),
        P(("gx", "gy"), None),
        P(("gx", "gy"), None, None, None),
        P(("gx", "gy"), None),
        P(("gx", "gy"), None, None),
        P(),
    )
    return jax.shard_map(body, mesh=mesh, in_specs=placed, out_specs=P("gx", "gy"), check_vma=False)
```

```python
import jax
import jax.numpy as jnp
from jax import lax
from jax.sharding import PartitionSpec as P

DEG = 6
W = 64
CX = 2
CY = 1
CZ = 2
FILTERS = 2
ZN = 12
CAP = 2


PRECISE = lax.Precision.HIGHEST
DENSE = lax.Precision.HIGH


def shifted(value, axis, steps):
    count = lax.axis_size(axis)
    pairs = [(source, (source + steps) % count) for source in range(count)]
    return lax.ppermute(value, axis, pairs)


def diagonal(value, steps):
    count_x = lax.axis_size("gx")
    count_y = lax.axis_size("gy")
    pairs = [
        (u * count_y + v, ((u + steps) % count_x) * count_y + (v + steps) % count_y)
        for u in range(count_x)
        for v in range(count_y)
    ]
    return lax.ppermute(value, ("gx", "gy"), pairs)


def cell_ranges():
    for p in range(CX):
        for q in range(CY):
            for r in range(CZ):
                yield p * DEG, q * DEG, r * DEG


def gather_cells(extended):
    closed = jnp.concatenate([extended, extended[:, :, :1]], axis=2)
    blocks = [
        closed[x0 : x0 + DEG + 1, y0 : y0 + DEG + 1, z0 : z0 + DEG + 1]
        for x0, y0, z0 in cell_ranges()
    ]
    stacked = jnp.stack(blocks, axis=3)
    return stacked.reshape((DEG + 1) ** 3, len(blocks) * stacked.shape[-1])


def scatter_cells(cell_out, columns):
    cells = cell_out.shape[1] // columns
    blocks = cell_out.reshape(DEG + 1, DEG + 1, DEG + 1, cells, columns)
    nx, ny, nz = CX * DEG + 1, CY * DEG + 1, CZ * DEG + 1
    total = None
    for index, (x0, y0, z0) in enumerate(cell_ranges()):
        padded = jnp.pad(
            blocks[:, :, :, index],
            ((x0, nx - x0 - DEG - 1), (y0, ny - y0 - DEG - 1), (z0, nz - z0 - DEG - 1), (0, 0)),
        )
        total = padded if total is None else total + padded
    return total[:, :, :ZN].at[:, :, 0].add(total[:, :, ZN])


def body(wavefunctions, potential, cell_matrix, pair_cell, pair_tile, slot_atom, coupling, bounds):
    rows_x = wavefunctions.shape[0]
    rows_y = potential.shape[1] // ZN
    slots, nproj, npc = pair_tile.shape[1:]
    atoms = coupling.shape[0]
    cells = CX * CY * CZ
    owners = lax.axis_size(("gx", "gy"))
    local_pot = potential.reshape(rows_x, rows_y, ZN, 1)
    cell_mask = (pair_cell[0][:, None] == jnp.arange(cells, dtype=jnp.int32)[None, :]).astype(jnp.float32)
    one_hot = (
        slot_atom[0][:, None] == jnp.arange(atoms, dtype=jnp.int32)[None, :]
    ).astype(jnp.float32)
    rows = -(-nproj // 8) * 8
    tile_all = jnp.pad(pair_tile[0], ((0, 0), (0, rows - nproj), (0, 0))).reshape(slots * rows, npc)
    tile_t = tile_all.T
    mask_all = jnp.repeat(cell_mask, rows, axis=0)
    incoming = one_hot.reshape(owners, CAP, atoms)
    hot_k = [incoming[:, k] for k in range(CAP)]
    coupling_pad = jnp.pad(coupling, ((0, 0), (0, rows - nproj), (0, rows - nproj)))

    def exchange(values):
        return lax.all_to_all(values, ("gx", "gy"), split_axis=0, concat_axis=0, tiled=True)

    def owner_work(received):
        atom_sums = None
        for k in range(CAP):
            full = jnp.einsum("sa,spx->apx", hot_k[k], received, precision=PRECISE)
            part = full[:, :, k * W : (k + 1) * W]
            atom_sums = part if atom_sums is None else atom_sums + part
        applied = jnp.einsum("apq,aqw->apw", coupling_pad, atom_sums, precision=PRECISE)
        return jnp.concatenate(
            [jnp.einsum("sa,apw->spw", hot_k[k], applied, precision=PRECISE) for k in range(CAP)],
            axis=-1,
        )

    def apply_operator(current):
        face_x = shifted(current[:1], "gx", -1)
        face_y = shifted(current[:, :1], "gy", -1)
        corner = diagonal(current[:1, :1], -1)
        extended = jnp.concatenate(
            [
                jnp.concatenate([current, face_y], axis=1),
                jnp.concatenate([face_x, corner], axis=1),
            ],
            axis=0,
        )
        cell_in = gather_cells(extended)
        every_cell = jnp.dot(tile_all, cell_in, precision=DENSE)
        picked = None
        for c in range(cells):
            term = every_cell[:, c * W : (c + 1) * W] * mask_all[:, c : c + 1]
            picked = term if picked is None else picked + term
        picked = picked.reshape(owners, CAP, rows, W)
        send = jnp.concatenate([picked[:, k] for k in range(CAP)], axis=-1)
        returned = exchange(owner_work(exchange(send)))
        by_slot = jnp.stack(
            [returned[:, :, k * W : (k + 1) * W] for k in range(CAP)], axis=1
        ).reshape(slots * rows, W)
        spread_in = jnp.concatenate([by_slot * mask_all[:, c : c + 1] for c in range(cells)], axis=1)
        spread = jnp.dot(cell_matrix, cell_in, precision=DENSE) + jnp.dot(
            tile_t, spread_in, precision=DENSE
        )
        summed = scatter_cells(spread, W)
        from_y = shifted(summed[:rows_x, rows_y], "gy", 1)
        from_x = shifted(summed[rows_x, :rows_y], "gx", 1)
        from_corner = diagonal(summed[rows_x, rows_y], 1)
        summed = summed[:rows_x, :rows_y].at[:, 0].add(from_y)
        summed = summed.at[0].add(from_x).at[0, 0].add(from_corner)
        return summed + local_pot * current

    previous = wavefunctions.reshape(rows_x, rows_y, ZN, W)
    for filter_index in range(FILTERS):
        lower_bound = bounds[filter_index, 0]
        low_end = bounds[filter_index, 1]
        high_end = bounds[filter_index, 2]
        half_width = (high_end - low_end) / 2.0
        centre = (high_end + low_end) / 2.0
        sigma_now = half_width / (lower_bound - centre)
        gamma_term = 2.0 / sigma_now
        current = sigma_now / half_width * (apply_operator(previous) - centre * previous)
        sigma_next = 1.0 / (gamma_term - sigma_now)
        following = (
            2.0 * sigma_next / half_width * (apply_operator(current) - centre * current)
            - sigma_now * sigma_next * previous
        )
        current = following
        sigma_now = sigma_next
        previous = current
    return previous.reshape(rows_x, rows_y * ZN * W)


def solution(mesh):
    placed = (
        P("gx", "gy"),
        P("gx", "gy"),
        P(),
        P(("gx", "gy"), None),
        P(("gx", "gy"), None, None, None),
        P(("gx", "gy"), None),
        P(("gx", "gy"), None, None),
        P(),
    )
    return jax.shard_map(body, mesh=mesh, in_specs=placed, out_specs=P("gx", "gy"), check_vma=False)
```

```python
import jax
import jax.numpy as jnp
from jax import lax
from jax.sharding import PartitionSpec as P

DEG = 6
W = 64
CX = 2
CY = 1
CZ = 2
FILTERS = 2
ZN = 12
CAP = 2


PRECISE = lax.Precision.HIGHEST
DENSE = lax.Precision.HIGH


def shifted(value, axis, steps):
    count = lax.axis_size(axis)
    pairs = [(source, (source + steps) % count) for source in range(count)]
    return lax.ppermute(value, axis, pairs)


def diagonal(value, steps):
    count_x = lax.axis_size("gx")
    count_y = lax.axis_size("gy")
    pairs = [
        (u * count_y + v, ((u + steps) % count_x) * count_y + (v + steps) % count_y)
        for u in range(count_x)
        for v in range(count_y)
    ]
    return lax.ppermute(value, ("gx", "gy"), pairs)


def neighbour(value, dx, dy):
    count_x = lax.axis_size("gx")
    count_y = lax.axis_size("gy")
    pairs = [
        (u * count_y + v, ((u - dx) % count_x) * count_y + (v - dy) % count_y)
        for u in range(count_x)
        for v in range(count_y)
    ]
    return lax.ppermute(value, ("gx", "gy"), pairs)


def extend(values):
    face_x = neighbour(values[:1], 1, 0)
    face_y = neighbour(values[:, :1], 0, 1)
    corner = neighbour(values[:1, :1], 1, 1)
    return jnp.concatenate(
        [jnp.concatenate([values, face_y], axis=1), jnp.concatenate([face_x, corner], axis=1)],
        axis=0,
    )


def combine(partial, rows_x, rows_y):
    from_xm = neighbour(partial[rows_x], -1, 0)
    from_xp = neighbour(partial[0], 1, 0)
    from_ym = neighbour(partial[:, rows_y], 0, -1)
    from_yp = neighbour(partial[:, 0], 0, 1)
    corner_mm = neighbour(partial[rows_x, rows_y], -1, -1)
    corner_mp = neighbour(partial[rows_x, 0], -1, 1)
    corner_pm = neighbour(partial[0, rows_y], 1, -1)
    corner_pp = neighbour(partial[0, 0], 1, 1)
    total = partial.at[0].add(from_xm).at[rows_x].add(from_xp)
    total = total.at[:, 0].add(from_ym).at[:, rows_y].add(from_yp)
    total = total.at[0, 0].add(corner_mm).at[0, rows_y].add(corner_mp)
    return total.at[rows_x, 0].add(corner_pm).at[rows_x, rows_y].add(corner_pp)


def cell_ranges():
    for p in range(CX):
        for q in range(CY):
            for r in range(CZ):
                yield p * DEG, q * DEG, r * DEG


def gather_cells(extended):
    closed = jnp.concatenate([extended, extended[:, :, :1]], axis=2)
    blocks = [
        closed[x0 : x0 + DEG + 1, y0 : y0 + DEG + 1, z0 : z0 + DEG + 1]
        for x0, y0, z0 in cell_ranges()
    ]
    stacked = jnp.stack(blocks, axis=3)
    return stacked.reshape((DEG + 1) ** 3, len(blocks) * stacked.shape[-1])


def scatter_cells(cell_out, columns):
    cells = cell_out.shape[1] // columns
    blocks = cell_out.reshape(DEG + 1, DEG + 1, DEG + 1, cells, columns)
    nx, ny, nz = CX * DEG + 1, CY * DEG + 1, CZ * DEG + 1
    total = None
    for index, (x0, y0, z0) in enumerate(cell_ranges()):
        padded = jnp.pad(
            blocks[:, :, :, index],
            ((x0, nx - x0 - DEG - 1), (y0, ny - y0 - DEG - 1), (z0, nz - z0 - DEG - 1), (0, 0)),
        )
        total = padded if total is None else total + padded
    return total[:, :, :ZN].at[:, :, 0].add(total[:, :, ZN])


def body(wavefunctions, potential, cell_matrix, pair_cell, pair_tile, slot_atom, coupling, bounds):
    rows_x = wavefunctions.shape[0]
    rows_y = potential.shape[1] // ZN
    slots, nproj, npc = pair_tile.shape[1:]
    atoms = coupling.shape[0]
    cells = CX * CY * CZ
    owners = lax.axis_size(("gx", "gy"))
    local_pot = extend(potential.reshape(rows_x, rows_y, ZN, 1))
    cell_mask = (pair_cell[0][:, None] == jnp.arange(cells, dtype=jnp.int32)[None, :]).astype(jnp.float32)
    one_hot = (
        slot_atom[0][:, None] == jnp.arange(atoms, dtype=jnp.int32)[None, :]
    ).astype(jnp.float32)
    rows = -(-nproj // 8) * 8
    tile_all = jnp.pad(pair_tile[0], ((0, 0), (0, rows - nproj), (0, 0))).reshape(slots * rows, npc)
    tile_t = tile_all.T
    mask_all = jnp.repeat(cell_mask, rows, axis=0)
    incoming = one_hot.reshape(owners, CAP, atoms)
    hot_k = [incoming[:, k] for k in range(CAP)]
    coupling_pad = jnp.pad(coupling, ((0, 0), (0, rows - nproj), (0, rows - nproj)))

    def exchange(values):
        return lax.all_to_all(values, ("gx", "gy"), split_axis=0, concat_axis=0, tiled=True)

    def owner_work(received):
        atom_sums = None
        for k in range(CAP):
            full = jnp.einsum("sa,spx->apx", hot_k[k], received, precision=PRECISE)
            part = full[:, :, k * W : (k + 1) * W]
            atom_sums = part if atom_sums is None else atom_sums + part
        applied = jnp.einsum("apq,aqw->apw", coupling_pad, atom_sums, precision=PRECISE)
        return jnp.concatenate(
            [jnp.einsum("sa,apw->spw", hot_k[k], applied, precision=PRECISE) for k in range(CAP)],
            axis=-1,
        )

    def apply_operator(current):
        cell_in = gather_cells(current)
        every_cell = jnp.dot(tile_all, cell_in, precision=DENSE)
        picked = None
        for c in range(cells):
            term = every_cell[:, c * W : (c + 1) * W] * mask_all[:, c : c + 1]
            picked = term if picked is None else picked + term
        picked = picked.reshape(owners, CAP, rows, W)
        send = jnp.concatenate([picked[:, k] for k in range(CAP)], axis=-1)
        returned = exchange(owner_work(exchange(send)))
        by_slot = jnp.stack(
            [returned[:, :, k * W : (k + 1) * W] for k in range(CAP)], axis=1
        ).reshape(slots * rows, W)
        spread_in = jnp.concatenate([by_slot * mask_all[:, c : c + 1] for c in range(cells)], axis=1)
        spread = jnp.dot(cell_matrix, cell_in, precision=DENSE) + jnp.dot(
            tile_t, spread_in, precision=DENSE
        )
        summed = combine(scatter_cells(spread, W), rows_x, rows_y)
        return summed + local_pot * current

    previous = extend(wavefunctions.reshape(rows_x, rows_y, ZN, W))
    for filter_index in range(FILTERS):
        lower_bound = bounds[filter_index, 0]
        low_end = bounds[filter_index, 1]
        high_end = bounds[filter_index, 2]
        half_width = (high_end - low_end) / 2.0
        centre = (high_end + low_end) / 2.0
        sigma_now = half_width / (lower_bound - centre)
        gamma_term = 2.0 / sigma_now
        current = sigma_now / half_width * (apply_operator(previous) - centre * previous)
        sigma_next = 1.0 / (gamma_term - sigma_now)
        following = (
            2.0 * sigma_next / half_width * (apply_operator(current) - centre * current)
            - sigma_now * sigma_next * previous
        )
        current = following
        sigma_now = sigma_next
        previous = current
    return previous[:rows_x, :rows_y].reshape(rows_x, rows_y * ZN * W)


def solution(mesh):
    placed = (
        P("gx", "gy"),
        P("gx", "gy"),
        P(),
        P(("gx", "gy"), None),
        P(("gx", "gy"), None, None, None),
        P(("gx", "gy"), None),
        P(("gx", "gy"), None, None),
        P(),
    )
    return jax.shard_map(body, mesh=mesh, in_specs=placed, out_specs=P("gx", "gy"), check_vma=False)
```

```python
import jax
import jax.numpy as jnp
from jax import lax
from jax.sharding import PartitionSpec as P

DEG = 6
W = 64
CX = 2
CY = 1
CZ = 2
FILTERS = 2
ZN = 12
CAP = 2


PRECISE = lax.Precision.HIGHEST
DENSE = lax.Precision.HIGH


def shifted(value, axis, steps):
    count = lax.axis_size(axis)
    pairs = [(source, (source + steps) % count) for source in range(count)]
    return lax.ppermute(value, axis, pairs)


def diagonal(value, steps):
    count_x = lax.axis_size("gx")
    count_y = lax.axis_size("gy")
    pairs = [
        (u * count_y + v, ((u + steps) % count_x) * count_y + (v + steps) % count_y)
        for u in range(count_x)
        for v in range(count_y)
    ]
    return lax.ppermute(value, ("gx", "gy"), pairs)


def cell_ranges():
    for p in range(CX):
        for q in range(CY):
            for r in range(CZ):
                yield p * DEG, q * DEG, r * DEG


def gather_cells(extended):
    closed = jnp.concatenate([extended, extended[:, :, :1]], axis=2)
    blocks = [
        closed[x0 : x0 + DEG + 1, y0 : y0 + DEG + 1, z0 : z0 + DEG + 1]
        for x0, y0, z0 in cell_ranges()
    ]
    stacked = jnp.stack(blocks, axis=3)
    return stacked.reshape((DEG + 1) ** 3, len(blocks) * stacked.shape[-1])


def scatter_cells(cell_out, columns):
    cells = cell_out.shape[1] // columns
    blocks = cell_out.reshape(DEG + 1, DEG + 1, DEG + 1, cells, columns)
    nx, ny, nz = CX * DEG + 1, CY * DEG + 1, CZ * DEG + 1
    total = None
    for index, (x0, y0, z0) in enumerate(cell_ranges()):
        padded = jnp.pad(
            blocks[:, :, :, index],
            ((x0, nx - x0 - DEG - 1), (y0, ny - y0 - DEG - 1), (z0, nz - z0 - DEG - 1), (0, 0)),
        )
        total = padded if total is None else total + padded
    return total[:, :, :ZN].at[:, :, 0].add(total[:, :, ZN])


def body(wavefunctions, potential, cell_matrix, pair_cell, pair_tile, slot_atom, coupling, bounds):
    rows_x = wavefunctions.shape[0]
    rows_y = potential.shape[1] // ZN
    slots, nproj, npc = pair_tile.shape[1:]
    atoms = coupling.shape[0]
    cells = CX * CY * CZ
    owners = lax.axis_size(("gx", "gy"))
    local_pot = potential.reshape(rows_x, rows_y, ZN, 1)
    cell_mask = (pair_cell[0][:, None] == jnp.arange(cells, dtype=jnp.int32)[None, :]).astype(jnp.float32)
    one_hot = (
        slot_atom[0][:, None] == jnp.arange(atoms, dtype=jnp.int32)[None, :]
    ).astype(jnp.float32)
    rows = -(-nproj // 8) * 8
    tile_all = jnp.pad(pair_tile[0], ((0, 0), (0, rows - nproj), (0, 0))).reshape(slots * rows, npc)
    tile_t = tile_all.T
    mask_all = jnp.repeat(cell_mask, rows, axis=0)
    incoming = one_hot.reshape(owners, CAP, atoms)
    hot_k = [incoming[:, k] for k in range(CAP)]
    coupling_pad = jnp.pad(coupling, ((0, 0), (0, rows - nproj), (0, rows - nproj)))

    def exchange(values):
        return lax.all_to_all(values, ("gx", "gy"), split_axis=0, concat_axis=0, tiled=True)

    def owner_work(received):
        atom_sums = None
        for k in range(CAP):
            full = jnp.einsum("sa,spx->apx", hot_k[k], received, precision=PRECISE)
            part = full[:, :, k * W : (k + 1) * W]
            atom_sums = part if atom_sums is None else atom_sums + part
        applied = jnp.einsum("apq,aqw->apw", coupling_pad, atom_sums, precision=PRECISE)
        return jnp.concatenate(
            [jnp.einsum("sa,apw->spw", hot_k[k], applied, precision=PRECISE) for k in range(CAP)],
            axis=-1,
        )

    def apply_operator(current):
        face_x = shifted(current[:1], "gx", -1)
        face_y = shifted(current[:, :1], "gy", -1)
        corner = diagonal(current[:1, :1], -1)
        extended = jnp.concatenate(
            [
                jnp.concatenate([current, face_y], axis=1),
                jnp.concatenate([face_x, corner], axis=1),
            ],
            axis=0,
        )
        cell_in = gather_cells(extended)
        every_cell = jnp.dot(tile_all, cell_in, precision=DENSE)
        picked = None
        for c in range(cells):
            term = every_cell[:, c * W : (c + 1) * W] * mask_all[:, c : c + 1]
            picked = term if picked is None else picked + term
        picked = picked.reshape(owners, CAP, rows, W)
        send = jnp.concatenate([picked[:, k] for k in range(CAP)], axis=-1)
        kinetic = lax.optimization_barrier(jnp.dot(cell_matrix, cell_in, precision=DENSE))
        returned = exchange(owner_work(exchange(send)))
        by_slot = jnp.stack(
            [returned[:, :, k * W : (k + 1) * W] for k in range(CAP)], axis=1
        ).reshape(slots * rows, W)
        spread_in = jnp.concatenate([by_slot * mask_all[:, c : c + 1] for c in range(cells)], axis=1)
        spread = kinetic + jnp.dot(tile_t, spread_in, precision=DENSE)
        summed = scatter_cells(spread, W)
        from_y = shifted(summed[:rows_x, rows_y], "gy", 1)
        from_x = shifted(summed[rows_x, :rows_y], "gx", 1)
        from_corner = diagonal(summed[rows_x, rows_y], 1)
        summed = summed[:rows_x, :rows_y].at[:, 0].add(from_y)
        summed = summed.at[0].add(from_x).at[0, 0].add(from_corner)
        return summed + local_pot * current

    previous = wavefunctions.reshape(rows_x, rows_y, ZN, W)
    for filter_index in range(FILTERS):
        lower_bound = bounds[filter_index, 0]
        low_end = bounds[filter_index, 1]
        high_end = bounds[filter_index, 2]
        half_width = (high_end - low_end) / 2.0
        centre = (high_end + low_end) / 2.0
        sigma_now = half_width / (lower_bound - centre)
        gamma_term = 2.0 / sigma_now
        current = sigma_now / half_width * (apply_operator(previous) - centre * previous)
        sigma_next = 1.0 / (gamma_term - sigma_now)
        following = (
            2.0 * sigma_next / half_width * (apply_operator(current) - centre * current)
            - sigma_now * sigma_next * previous
        )
        current = following
        sigma_now = sigma_next
        previous = current
    return previous.reshape(rows_x, rows_y * ZN * W)


def solution(mesh):
    placed = (
        P("gx", "gy"),
        P("gx", "gy"),
        P(),
        P(("gx", "gy"), None),
        P(("gx", "gy"), None, None, None),
        P(("gx", "gy"), None),
        P(("gx", "gy"), None, None),
        P(),
    )
    return jax.shard_map(body, mesh=mesh, in_specs=placed, out_specs=P("gx", "gy"), check_vma=False)
```

```python
import jax
import jax.numpy as jnp
from jax import lax
from jax.sharding import PartitionSpec as P

DEG = 6
W = 64
CX = 2
CY = 1
CZ = 2
FILTERS = 2
ZN = 12
CAP = 2


PRECISE = lax.Precision.HIGHEST
DENSE = lax.Precision.HIGH


def shifted(value, axis, steps):
    count = lax.axis_size(axis)
    pairs = [(source, (source + steps) % count) for source in range(count)]
    return lax.ppermute(value, axis, pairs)


def diagonal(value, steps):
    count_x = lax.axis_size("gx")
    count_y = lax.axis_size("gy")
    pairs = [
        (u * count_y + v, ((u + steps) % count_x) * count_y + (v + steps) % count_y)
        for u in range(count_x)
        for v in range(count_y)
    ]
    return lax.ppermute(value, ("gx", "gy"), pairs)


def cell_ranges():
    for p in range(CX):
        for q in range(CY):
            for r in range(CZ):
                yield p * DEG, q * DEG, r * DEG


def gather_cells(extended):
    closed = jnp.concatenate([extended, extended[:, :, :1]], axis=2)
    blocks = [
        closed[x0 : x0 + DEG + 1, y0 : y0 + DEG + 1, z0 : z0 + DEG + 1]
        for x0, y0, z0 in cell_ranges()
    ]
    stacked = jnp.stack(blocks, axis=3)
    return stacked.reshape((DEG + 1) ** 3, len(blocks) * stacked.shape[-1])


def split_nodes(matrix):
    nodes = matrix.reshape(matrix.shape[0], DEG + 1, DEG + 1, DEG + 1)
    own = nodes[:, :DEG, :DEG].reshape(matrix.shape[0], -1)
    rim = jnp.concatenate(
        [nodes[:, DEG].reshape(matrix.shape[0], -1), nodes[:, :DEG, DEG].reshape(matrix.shape[0], -1)],
        axis=1,
    )
    return own, rim


def split_cells(current, extended):
    local = jnp.concatenate([current, current[:, :, :1]], axis=2)
    closed = jnp.concatenate([extended, extended[:, :, :1]], axis=2)
    own, rim_x, rim_y = [], [], []
    for x0, y0, z0 in cell_ranges():
        own.append(local[x0 : x0 + DEG, y0 : y0 + DEG, z0 : z0 + DEG + 1])
        rim_x.append(closed[x0 + DEG, y0 : y0 + DEG + 1, z0 : z0 + DEG + 1])
        rim_y.append(closed[x0 : x0 + DEG, y0 + DEG, z0 : z0 + DEG + 1])
    columns = len(own) * current.shape[-1]
    own = jnp.stack(own, axis=-2).reshape(-1, columns)
    rim = jnp.concatenate(
        [jnp.stack(rim_x, axis=-2).reshape(-1, columns), jnp.stack(rim_y, axis=-2).reshape(-1, columns)],
        axis=0,
    )
    return own, rim


def scatter_cells(cell_out, columns):
    cells = cell_out.shape[1] // columns
    blocks = cell_out.reshape(DEG + 1, DEG + 1, DEG + 1, cells, columns)
    nx, ny, nz = CX * DEG + 1, CY * DEG + 1, CZ * DEG + 1
    total = None
    for index, (x0, y0, z0) in enumerate(cell_ranges()):
        padded = jnp.pad(
            blocks[:, :, :, index],
            ((x0, nx - x0 - DEG - 1), (y0, ny - y0 - DEG - 1), (z0, nz - z0 - DEG - 1), (0, 0)),
        )
        total = padded if total is None else total + padded
    return total[:, :, :ZN].at[:, :, 0].add(total[:, :, ZN])


def body(wavefunctions, potential, cell_matrix, pair_cell, pair_tile, slot_atom, coupling, bounds):
    rows_x = wavefunctions.shape[0]
    rows_y = potential.shape[1] // ZN
    slots, nproj, npc = pair_tile.shape[1:]
    atoms = coupling.shape[0]
    cells = CX * CY * CZ
    owners = lax.axis_size(("gx", "gy"))
    local_pot = potential.reshape(rows_x, rows_y, ZN, 1)
    cell_mask = (pair_cell[0][:, None] == jnp.arange(cells, dtype=jnp.int32)[None, :]).astype(jnp.float32)
    one_hot = (
        slot_atom[0][:, None] == jnp.arange(atoms, dtype=jnp.int32)[None, :]
    ).astype(jnp.float32)
    rows = -(-nproj // 8) * 8
    tile_all = jnp.pad(pair_tile[0], ((0, 0), (0, rows - nproj), (0, 0))).reshape(slots * rows, npc)
    tile_t = tile_all.T
    own_tile, rim_tile = split_nodes(tile_all)
    own_kin, rim_kin = split_nodes(cell_matrix)
    mask_all = jnp.repeat(cell_mask, rows, axis=0)
    incoming = one_hot.reshape(owners, CAP, atoms)
    hot_k = [incoming[:, k] for k in range(CAP)]
    coupling_pad = jnp.pad(coupling, ((0, 0), (0, rows - nproj), (0, rows - nproj)))

    def exchange(values):
        return lax.all_to_all(values, ("gx", "gy"), split_axis=0, concat_axis=0, tiled=True)

    def owner_work(received):
        atom_sums = None
        for k in range(CAP):
            full = jnp.einsum("sa,spx->apx", hot_k[k], received, precision=PRECISE)
            part = full[:, :, k * W : (k + 1) * W]
            atom_sums = part if atom_sums is None else atom_sums + part
        applied = jnp.einsum("apq,aqw->apw", coupling_pad, atom_sums, precision=PRECISE)
        return jnp.concatenate(
            [jnp.einsum("sa,apw->spw", hot_k[k], applied, precision=PRECISE) for k in range(CAP)],
            axis=-1,
        )

    def apply_operator(current):
        face_x = shifted(current[:1], "gx", -1)
        face_y = shifted(current[:, :1], "gy", -1)
        corner = diagonal(current[:1, :1], -1)
        extended = jnp.concatenate(
            [
                jnp.concatenate([current, face_y], axis=1),
                jnp.concatenate([face_x, corner], axis=1),
            ],
            axis=0,
        )
        own_in, rim_in = split_cells(current, extended)
        every_cell = jnp.dot(own_tile, own_in, precision=DENSE) + jnp.dot(rim_tile, rim_in, precision=DENSE)
        picked = None
        for c in range(cells):
            term = every_cell[:, c * W : (c + 1) * W] * mask_all[:, c : c + 1]
            picked = term if picked is None else picked + term
        picked = picked.reshape(owners, CAP, rows, W)
        send = jnp.concatenate([picked[:, k] for k in range(CAP)], axis=-1)
        kinetic = jnp.dot(own_kin, own_in, precision=DENSE) + jnp.dot(rim_kin, rim_in, precision=DENSE)
        returned = exchange(owner_work(exchange(send)))
        by_slot = jnp.stack(
            [returned[:, :, k * W : (k + 1) * W] for k in range(CAP)], axis=1
        ).reshape(slots * rows, W)
        spread_in = jnp.concatenate([by_slot * mask_all[:, c : c + 1] for c in range(cells)], axis=1)
        spread = kinetic + jnp.dot(tile_t, spread_in, precision=DENSE)
        summed = scatter_cells(spread, W)
        from_y = shifted(summed[:rows_x, rows_y], "gy", 1)
        from_x = shifted(summed[rows_x, :rows_y], "gx", 1)
        from_corner = diagonal(summed[rows_x, rows_y], 1)
        summed = summed[:rows_x, :rows_y].at[:, 0].add(from_y)
        summed = summed.at[0].add(from_x).at[0, 0].add(from_corner)
        return summed + local_pot * current

    previous = wavefunctions.reshape(rows_x, rows_y, ZN, W)
    for filter_index in range(FILTERS):
        lower_bound = bounds[filter_index, 0]
        low_end = bounds[filter_index, 1]
        high_end = bounds[filter_index, 2]
        half_width = (high_end - low_end) / 2.0
        centre = (high_end + low_end) / 2.0
        sigma_now = half_width / (lower_bound - centre)
        gamma_term = 2.0 / sigma_now
        current = sigma_now / half_width * (apply_operator(previous) - centre * previous)
        sigma_next = 1.0 / (gamma_term - sigma_now)
        following = (
            2.0 * sigma_next / half_width * (apply_operator(current) - centre * current)
            - sigma_now * sigma_next * previous
        )
        current = following
        sigma_now = sigma_next
        previous = current
    return previous.reshape(rows_x, rows_y * ZN * W)


def solution(mesh):
    placed = (
        P("gx", "gy"),
        P("gx", "gy"),
        P(),
        P(("gx", "gy"), None),
        P(("gx", "gy"), None, None, None),
        P(("gx", "gy"), None),
        P(("gx", "gy"), None, None),
        P(),
    )
    return jax.shard_map(body, mesh=mesh, in_specs=placed, out_specs=P("gx", "gy"), check_vma=False)
```

```python
import jax
import jax.numpy as jnp
from jax import lax
from jax.sharding import PartitionSpec as P

DEG = 6
W = 64
CX = 2
CY = 1
CZ = 2
FILTERS = 2
ZN = 12
CAP = 2


PRECISE = lax.Precision.HIGHEST
DENSE = lax.Precision.HIGH


def shifted(value, axis, steps):
    count = lax.axis_size(axis)
    pairs = [(source, (source + steps) % count) for source in range(count)]
    return lax.ppermute(value, axis, pairs)


def diagonal(value, steps):
    count_x = lax.axis_size("gx")
    count_y = lax.axis_size("gy")
    pairs = [
        (u * count_y + v, ((u + steps) % count_x) * count_y + (v + steps) % count_y)
        for u in range(count_x)
        for v in range(count_y)
    ]
    return lax.ppermute(value, ("gx", "gy"), pairs)


def cell_ranges():
    for p in range(CX):
        for q in range(CY):
            for r in range(CZ):
                yield p * DEG, q * DEG, r * DEG


def gather_cells(extended):
    closed = jnp.concatenate([extended, extended[:, :, :1]], axis=2)
    blocks = [
        closed[x0 : x0 + DEG + 1, y0 : y0 + DEG + 1, z0 : z0 + DEG + 1]
        for x0, y0, z0 in cell_ranges()
    ]
    stacked = jnp.stack(blocks, axis=3)
    return stacked.reshape((DEG + 1) ** 3, len(blocks) * stacked.shape[-1])


def scatter_cells(cell_out, columns):
    cells = cell_out.shape[1] // columns
    blocks = cell_out.reshape(DEG + 1, DEG + 1, DEG + 1, cells, columns)
    nx, ny, nz = CX * DEG + 1, CY * DEG + 1, CZ * DEG + 1
    total = None
    for index, (x0, y0, z0) in enumerate(cell_ranges()):
        padded = jnp.pad(
            blocks[:, :, :, index],
            ((x0, nx - x0 - DEG - 1), (y0, ny - y0 - DEG - 1), (z0, nz - z0 - DEG - 1), (0, 0)),
        )
        total = padded if total is None else total + padded
    return total[:, :, :ZN].at[:, :, 0].add(total[:, :, ZN])


def body(wavefunctions, potential, cell_matrix, pair_cell, pair_tile, slot_atom, coupling, bounds):
    rows_x = wavefunctions.shape[0]
    rows_y = potential.shape[1] // ZN
    slots, nproj, npc = pair_tile.shape[1:]
    atoms = coupling.shape[0]
    cells = CX * CY * CZ
    owners = lax.axis_size(("gx", "gy"))
    local_pot = potential.reshape(rows_x, rows_y, ZN, 1)
    cell_mask = (pair_cell[0][:, None] == jnp.arange(cells, dtype=jnp.int32)[None, :]).astype(jnp.float32)
    one_hot = (
        slot_atom[0][:, None] == jnp.arange(atoms, dtype=jnp.int32)[None, :]
    ).astype(jnp.float32)
    rows = -(-nproj // 8) * 8
    by_pair = pair_tile[0].reshape(owners, CAP, nproj, npc).transpose(1, 0, 2, 3)
    tile_all = jnp.pad(by_pair, ((0, 0), (0, 0), (0, rows - nproj), (0, 0))).reshape(slots * rows, npc)
    tile_t = tile_all.T
    pair_mask = cell_mask.reshape(owners, CAP, cells).transpose(1, 0, 2).reshape(slots, cells)
    mask_all = jnp.repeat(pair_mask, rows, axis=0)
    incoming = one_hot.reshape(owners, CAP, atoms)
    hot_k = [incoming[:, k] for k in range(CAP)]
    coupling_pad = jnp.pad(coupling, ((0, 0), (0, rows - nproj), (0, rows - nproj)))

    def exchange(values):
        return lax.all_to_all(values, ("gx", "gy"), split_axis=0, concat_axis=0, tiled=True)

    def owner_work(received):
        atom_sums = None
        for k in range(CAP):
            full = jnp.einsum("sa,spx->apx", hot_k[k], received, precision=PRECISE)
            part = full[:, :, k * W : (k + 1) * W]
            atom_sums = part if atom_sums is None else atom_sums + part
        applied = jnp.einsum("apq,aqw->apw", coupling_pad, atom_sums, precision=PRECISE)
        return jnp.concatenate(
            [jnp.einsum("sa,apw->spw", hot_k[k], applied, precision=PRECISE) for k in range(CAP)],
            axis=-1,
        )

    def apply_operator(current):
        face_x = shifted(current[:1], "gx", -1)
        face_y = shifted(current[:, :1], "gy", -1)
        corner = diagonal(current[:1, :1], -1)
        extended = jnp.concatenate(
            [
                jnp.concatenate([current, face_y], axis=1),
                jnp.concatenate([face_x, corner], axis=1),
            ],
            axis=0,
        )
        cell_in = gather_cells(extended)
        every_cell = jnp.dot(tile_all, cell_in, precision=DENSE)
        picked = None
        for c in range(cells):
            term = every_cell[:, c * W : (c + 1) * W] * mask_all[:, c : c + 1]
            picked = term if picked is None else picked + term
        picked = picked.reshape(CAP, owners, rows, W)
        send = jnp.concatenate([picked[k] for k in range(CAP)], axis=-1)
        returned = exchange(owner_work(exchange(send)))
        by_slot = jnp.concatenate(
            [returned[:, :, k * W : (k + 1) * W] for k in range(CAP)], axis=0
        ).reshape(slots * rows, W)
        spread_in = jnp.concatenate([by_slot * mask_all[:, c : c + 1] for c in range(cells)], axis=1)
        spread = jnp.dot(cell_matrix, cell_in, precision=DENSE) + jnp.dot(
            tile_t, spread_in, precision=DENSE
        )
        summed = scatter_cells(spread, W)
        from_y = shifted(summed[:rows_x, rows_y], "gy", 1)
        from_x = shifted(summed[rows_x, :rows_y], "gx", 1)
        from_corner = diagonal(summed[rows_x, rows_y], 1)
        summed = summed[:rows_x, :rows_y].at[:, 0].add(from_y)
        summed = summed.at[0].add(from_x).at[0, 0].add(from_corner)
        return summed + local_pot * current

    previous = wavefunctions.reshape(rows_x, rows_y, ZN, W)
    for filter_index in range(FILTERS):
        lower_bound = bounds[filter_index, 0]
        low_end = bounds[filter_index, 1]
        high_end = bounds[filter_index, 2]
        half_width = (high_end - low_end) / 2.0
        centre = (high_end + low_end) / 2.0
        sigma_now = half_width / (lower_bound - centre)
        gamma_term = 2.0 / sigma_now
        current = sigma_now / half_width * (apply_operator(previous) - centre * previous)
        sigma_next = 1.0 / (gamma_term - sigma_now)
        following = (
            2.0 * sigma_next / half_width * (apply_operator(current) - centre * current)
            - sigma_now * sigma_next * previous
        )
        current = following
        sigma_now = sigma_next
        previous = current
    return previous.reshape(rows_x, rows_y * ZN * W)


def solution(mesh):
    placed = (
        P("gx", "gy"),
        P("gx", "gy"),
        P(),
        P(("gx", "gy"), None),
        P(("gx", "gy"), None, None, None),
        P(("gx", "gy"), None),
        P(("gx", "gy"), None, None),
        P(),
    )
    return jax.shard_map(body, mesh=mesh, in_specs=placed, out_specs=P("gx", "gy"), check_vma=False)
```

```python
import jax
import jax.numpy as jnp
from jax import lax
from jax.sharding import PartitionSpec as P

DEG = 6
W = 64
CX = 2
CY = 1
CZ = 2
FILTERS = 2
ZN = 12
CAP = 2


PRECISE = lax.Precision.HIGHEST
DENSE = lax.Precision.HIGH


def shifted(value, axis, steps):
    count = lax.axis_size(axis)
    pairs = [(source, (source + steps) % count) for source in range(count)]
    return lax.ppermute(value, axis, pairs)


def diagonal(value, steps):
    count_x = lax.axis_size("gx")
    count_y = lax.axis_size("gy")
    pairs = [
        (u * count_y + v, ((u + steps) % count_x) * count_y + (v + steps) % count_y)
        for u in range(count_x)
        for v in range(count_y)
    ]
    return lax.ppermute(value, ("gx", "gy"), pairs)


def cell_ranges():
    for p in range(CX):
        for q in range(CY):
            for r in range(CZ):
                yield p * DEG, q * DEG, r * DEG


def gather_cells(extended):
    closed = jnp.concatenate([extended, extended[:, :, :1]], axis=2)
    blocks = [
        closed[x0 : x0 + DEG + 1, y0 : y0 + DEG + 1, z0 : z0 + DEG + 1]
        for x0, y0, z0 in cell_ranges()
    ]
    stacked = jnp.stack(blocks, axis=3)
    return stacked.reshape((DEG + 1) ** 3, len(blocks) * stacked.shape[-1])


def scatter_cells(cell_out, columns):
    cells = cell_out.shape[1] // columns
    blocks = cell_out.reshape(DEG + 1, DEG + 1, DEG + 1, cells, columns)
    nx, ny = CX * DEG + 1, CY * DEG + 1
    total = None
    for index, (x0, y0, z0) in enumerate(cell_ranges()):
        block = blocks[:, :, :, index]
        spans = ((x0, nx - x0 - DEG - 1), (y0, ny - y0 - DEG - 1))
        if z0 + DEG < ZN:
            pieces = [jnp.pad(block, spans + ((z0, ZN - z0 - DEG - 1), (0, 0)))]
        else:
            pieces = [
                jnp.pad(block[:, :, :DEG], spans + ((z0, ZN - z0 - DEG), (0, 0))),
                jnp.pad(block[:, :, DEG:], spans + ((0, ZN - 1), (0, 0))),
            ]
        for padded in pieces:
            total = padded if total is None else total + padded
    return total


def body(wavefunctions, potential, cell_matrix, pair_cell, pair_tile, slot_atom, coupling, bounds):
    rows_x = wavefunctions.shape[0]
    rows_y = potential.shape[1] // ZN
    slots, nproj, npc = pair_tile.shape[1:]
    atoms = coupling.shape[0]
    cells = CX * CY * CZ
    owners = lax.axis_size(("gx", "gy"))
    local_pot = potential.reshape(rows_x, rows_y, ZN, 1)
    cell_mask = (pair_cell[0][:, None] == jnp.arange(cells, dtype=jnp.int32)[None, :]).astype(jnp.float32)
    one_hot = (
        slot_atom[0][:, None] == jnp.arange(atoms, dtype=jnp.int32)[None, :]
    ).astype(jnp.float32)
    rows = -(-nproj // 8) * 8
    tile_all = jnp.pad(pair_tile[0], ((0, 0), (0, rows - nproj), (0, 0))).reshape(slots * rows, npc)
    tile_t = tile_all.T
    mask_all = jnp.repeat(cell_mask, rows, axis=0)
    incoming = one_hot.reshape(owners, CAP, atoms)
    hot_k = [incoming[:, k] for k in range(CAP)]
    coupling_pad = jnp.pad(coupling, ((0, 0), (0, rows - nproj), (0, rows - nproj)))

    def exchange(values):
        return lax.all_to_all(values, ("gx", "gy"), split_axis=0, concat_axis=0, tiled=True)

    def owner_work(received):
        atom_sums = None
        for k in range(CAP):
            full = jnp.einsum("sa,spx->apx", hot_k[k], received, precision=PRECISE)
            part = full[:, :, k * W : (k + 1) * W]
            atom_sums = part if atom_sums is None else atom_sums + part
        applied = jnp.einsum("apq,aqw->apw", coupling_pad, atom_sums, precision=PRECISE)
        return jnp.concatenate(
            [jnp.einsum("sa,apw->spw", hot_k[k], applied, precision=PRECISE) for k in range(CAP)],
            axis=-1,
        )

    def apply_operator(current):
        face_x = shifted(current[:1], "gx", -1)
        face_y = shifted(current[:, :1], "gy", -1)
        corner = diagonal(current[:1, :1], -1)
        extended = jnp.concatenate(
            [
                jnp.concatenate([current, face_y], axis=1),
                jnp.concatenate([face_x, corner], axis=1),
            ],
            axis=0,
        )
        cell_in = gather_cells(extended)
        every_cell = jnp.dot(tile_all, cell_in, precision=DENSE)
        picked = None
        for c in range(cells):
            term = every_cell[:, c * W : (c + 1) * W] * mask_all[:, c : c + 1]
            picked = term if picked is None else picked + term
        picked = picked.reshape(owners, CAP, rows, W)
        send = jnp.concatenate([picked[:, k] for k in range(CAP)], axis=-1)
        returned = exchange(owner_work(exchange(send)))
        by_slot = jnp.stack(
            [returned[:, :, k * W : (k + 1) * W] for k in range(CAP)], axis=1
        ).reshape(slots * rows, W)
        spread_in = jnp.concatenate([by_slot * mask_all[:, c : c + 1] for c in range(cells)], axis=1)
        spread = jnp.dot(cell_matrix, cell_in, precision=DENSE) + jnp.dot(
            tile_t, spread_in, precision=DENSE
        )
        summed = scatter_cells(spread, W)
        from_y = shifted(summed[:rows_x, rows_y], "gy", 1)
        from_x = shifted(summed[rows_x, :rows_y], "gx", 1)
        from_corner = diagonal(summed[rows_x, rows_y], 1)
        summed = summed[:rows_x, :rows_y].at[:, 0].add(from_y)
        summed = summed.at[0].add(from_x).at[0, 0].add(from_corner)
        return summed + local_pot * current

    previous = wavefunctions.reshape(rows_x, rows_y, ZN, W)
    for filter_index in range(FILTERS):
        lower_bound = bounds[filter_index, 0]
        low_end = bounds[filter_index, 1]
        high_end = bounds[filter_index, 2]
        half_width = (high_end - low_end) / 2.0
        centre = (high_end + low_end) / 2.0
        sigma_now = half_width / (lower_bound - centre)
        gamma_term = 2.0 / sigma_now
        current = sigma_now / half_width * (apply_operator(previous) - centre * previous)
        sigma_next = 1.0 / (gamma_term - sigma_now)
        following = (
            2.0 * sigma_next / half_width * (apply_operator(current) - centre * current)
            - sigma_now * sigma_next * previous
        )
        current = following
        sigma_now = sigma_next
        previous = current
    return previous.reshape(rows_x, rows_y * ZN * W)


def solution(mesh):
    placed = (
        P("gx", "gy"),
        P("gx", "gy"),
        P(),
        P(("gx", "gy"), None),
        P(("gx", "gy"), None, None, None),
        P(("gx", "gy"), None),
        P(("gx", "gy"), None, None),
        P(),
    )
    return jax.shard_map(body, mesh=mesh, in_specs=placed, out_specs=P("gx", "gy"), check_vma=False)
```

```python
import jax
import jax.numpy as jnp
from jax import lax
from jax.sharding import PartitionSpec as P

DEG = 6
W = 64
CX = 2
CY = 1
CZ = 2
FILTERS = 2
ZN = 12
CAP = 2


PRECISE = lax.Precision.HIGHEST
DENSE = lax.Precision.HIGH


def shifted(value, axis, steps):
    count = lax.axis_size(axis)
    pairs = [(source, (source + steps) % count) for source in range(count)]
    return lax.ppermute(value, axis, pairs)


def diagonal(value, steps):
    count_x = lax.axis_size("gx")
    count_y = lax.axis_size("gy")
    pairs = [
        (u * count_y + v, ((u + steps) % count_x) * count_y + (v + steps) % count_y)
        for u in range(count_x)
        for v in range(count_y)
    ]
    return lax.ppermute(value, ("gx", "gy"), pairs)


def cell_ranges():
    for p in range(CX):
        for q in range(CY):
            for r in range(CZ):
                yield p * DEG, q * DEG, r * DEG


def gather_cells(extended):
    closed = jnp.concatenate([extended, extended[:, :, :1]], axis=2)
    blocks = [
        closed[x0 : x0 + DEG + 1, y0 : y0 + DEG + 1, z0 : z0 + DEG + 1]
        for x0, y0, z0 in cell_ranges()
    ]
    return jnp.concatenate(blocks, axis=-1).reshape((DEG + 1) ** 3, -1)


def scatter_cells(cell_out, columns):
    cells = cell_out.shape[1] // columns
    blocks = cell_out.reshape(DEG + 1, DEG + 1, DEG + 1, cells, columns)
    nx, ny = CX * DEG + 1, CY * DEG + 1
    total = None
    for index, (x0, y0, z0) in enumerate(cell_ranges()):
        block = blocks[:, :, :, index]
        spans = ((x0, nx - x0 - DEG - 1), (y0, ny - y0 - DEG - 1))
        if z0 + DEG < ZN:
            pieces = [jnp.pad(block, spans + ((z0, ZN - z0 - DEG - 1), (0, 0)))]
        else:
            pieces = [
                jnp.pad(block[:, :, :DEG], spans + ((z0, ZN - z0 - DEG), (0, 0))),
                jnp.pad(block[:, :, DEG:], spans + ((0, ZN - 1), (0, 0))),
            ]
        for padded in pieces:
            total = padded if total is None else total + padded
    return total


def body(wavefunctions, potential, cell_matrix, pair_cell, pair_tile, slot_atom, coupling, bounds):
    rows_x = wavefunctions.shape[0]
    rows_y = potential.shape[1] // ZN
    slots, nproj, npc = pair_tile.shape[1:]
    atoms = coupling.shape[0]
    cells = CX * CY * CZ
    owners = lax.axis_size(("gx", "gy"))
    local_pot = potential.reshape(rows_x, rows_y, ZN, 1)
    cell_mask = (pair_cell[0][:, None] == jnp.arange(cells, dtype=jnp.int32)[None, :]).astype(jnp.float32)
    one_hot = (
        slot_atom[0][:, None] == jnp.arange(atoms, dtype=jnp.int32)[None, :]
    ).astype(jnp.float32)
    rows = -(-nproj // 8) * 8
    tile_all = jnp.pad(pair_tile[0], ((0, 0), (0, rows - nproj), (0, 0))).reshape(slots * rows, npc)
    tile_t = tile_all.T
    mask_all = jnp.repeat(cell_mask, rows, axis=0)
    incoming = one_hot.reshape(owners, CAP, atoms)
    hot_k = [incoming[:, k] for k in range(CAP)]
    coupling_pad = jnp.pad(coupling, ((0, 0), (0, rows - nproj), (0, rows - nproj)))

    def exchange(values):
        return lax.all_to_all(values, ("gx", "gy"), split_axis=0, concat_axis=0, tiled=True)

    def owner_work(received):
        atom_sums = None
        for k in range(CAP):
            full = jnp.einsum("sa,spx->apx", hot_k[k], received, precision=PRECISE)
            part = full[:, :, k * W : (k + 1) * W]
            atom_sums = part if atom_sums is None else atom_sums + part
        applied = jnp.einsum("apq,aqw->apw", coupling_pad, atom_sums, precision=PRECISE)
        return jnp.concatenate(
            [jnp.einsum("sa,apw->spw", hot_k[k], applied, precision=PRECISE) for k in range(CAP)],
            axis=-1,
        )

    def apply_operator(current):
        face_x = shifted(current[:1], "gx", -1)
        face_y = shifted(current[:, :1], "gy", -1)
        corner = diagonal(current[:1, :1], -1)
        extended = jnp.concatenate(
            [
                jnp.concatenate([current, face_y], axis=1),
                jnp.concatenate([face_x, corner], axis=1),
            ],
            axis=0,
        )
        cell_in = gather_cells(extended)
        every_cell = jnp.dot(tile_all, cell_in, precision=DENSE)
        picked = None
        for c in range(cells):
            term = every_cell[:, c * W : (c + 1) * W] * mask_all[:, c : c + 1]
            picked = term if picked is None else picked + term
        picked = picked.reshape(owners, CAP, rows, W)
        send = jnp.concatenate([picked[:, k] for k in range(CAP)], axis=-1)
        returned = exchange(owner_work(exchange(send)))
        by_slot = jnp.stack(
            [returned[:, :, k * W : (k + 1) * W] for k in range(CAP)], axis=1
        ).reshape(slots * rows, W)
        spread_in = jnp.concatenate([by_slot * mask_all[:, c : c + 1] for c in range(cells)], axis=1)
        spread = jnp.dot(cell_matrix, cell_in, precision=DENSE) + jnp.dot(
            tile_t, spread_in, precision=DENSE
        )
        summed = scatter_cells(spread, W)
        from_y = shifted(summed[:rows_x, rows_y], "gy", 1)
        from_x = shifted(summed[rows_x, :rows_y], "gx", 1)
        from_corner = diagonal(summed[rows_x, rows_y], 1)
        summed = summed[:rows_x, :rows_y].at[:, 0].add(from_y)
        summed = summed.at[0].add(from_x).at[0, 0].add(from_corner)
        return summed + local_pot * current

    previous = wavefunctions.reshape(rows_x, rows_y, ZN, W)
    for filter_index in range(FILTERS):
        lower_bound = bounds[filter_index, 0]
        low_end = bounds[filter_index, 1]
        high_end = bounds[filter_index, 2]
        half_width = (high_end - low_end) / 2.0
        centre = (high_end + low_end) / 2.0
        sigma_now = half_width / (lower_bound - centre)
        gamma_term = 2.0 / sigma_now
        current = sigma_now / half_width * (apply_operator(previous) - centre * previous)
        sigma_next = 1.0 / (gamma_term - sigma_now)
        following = (
            2.0 * sigma_next / half_width * (apply_operator(current) - centre * current)
            - sigma_now * sigma_next * previous
        )
        current = following
        sigma_now = sigma_next
        previous = current
    return previous.reshape(rows_x, rows_y * ZN * W)


def solution(mesh):
    placed = (
        P("gx", "gy"),
        P("gx", "gy"),
        P(),
        P(("gx", "gy"), None),
        P(("gx", "gy"), None, None, None),
        P(("gx", "gy"), None),
        P(("gx", "gy"), None, None),
        P(),
    )
    return jax.shard_map(body, mesh=mesh, in_specs=placed, out_specs=P("gx", "gy"), check_vma=False)
```

```python
import jax
import jax.numpy as jnp
from jax import lax
from jax.sharding import PartitionSpec as P

DEG = 6
W = 64
CX = 2
CY = 1
CZ = 2
FILTERS = 2
ZN = 12
CAP = 2


PRECISE = lax.Precision.HIGHEST
DENSE = lax.Precision.HIGH


def shifted(value, axis, steps):
    count = lax.axis_size(axis)
    pairs = [(source, (source + steps) % count) for source in range(count)]
    return lax.ppermute(value, axis, pairs)


def diagonal(value, steps):
    count_x = lax.axis_size("gx")
    count_y = lax.axis_size("gy")
    pairs = [
        (u * count_y + v, ((u + steps) % count_x) * count_y + (v + steps) % count_y)
        for u in range(count_x)
        for v in range(count_y)
    ]
    return lax.ppermute(value, ("gx", "gy"), pairs)


def cell_ranges():
    for p in range(CX):
        for q in range(CY):
            for r in range(CZ):
                yield p * DEG, q * DEG, r * DEG


def gather_cells(extended):
    closed = jnp.concatenate([extended, extended[:, :, :1]], axis=2)
    blocks = [
        closed[x0 : x0 + DEG + 1, y0 : y0 + DEG + 1, z0 : z0 + DEG + 1]
        for x0, y0, z0 in cell_ranges()
    ]
    return jnp.concatenate(blocks, axis=-1).reshape((DEG + 1) ** 3, -1)


def scatter_cells(cell_out, columns):
    nx, ny = CX * DEG + 1, CY * DEG + 1
    total = None
    for index, (x0, y0, z0) in enumerate(cell_ranges()):
        block = cell_out[:, index * columns : (index + 1) * columns].reshape(DEG + 1, DEG + 1, DEG + 1, columns)
        spans = ((x0, nx - x0 - DEG - 1), (y0, ny - y0 - DEG - 1))
        if z0 + DEG < ZN:
            pieces = [jnp.pad(block, spans + ((z0, ZN - z0 - DEG - 1), (0, 0)))]
        else:
            pieces = [
                jnp.pad(block[:, :, :DEG], spans + ((z0, ZN - z0 - DEG), (0, 0))),
                jnp.pad(block[:, :, DEG:], spans + ((0, ZN - 1), (0, 0))),
            ]
        for padded in pieces:
            total = padded if total is None else total + padded
    return total


def body(wavefunctions, potential, cell_matrix, pair_cell, pair_tile, slot_atom, coupling, bounds):
    rows_x = wavefunctions.shape[0]
    rows_y = potential.shape[1] // ZN
    slots, nproj, npc = pair_tile.shape[1:]
    atoms = coupling.shape[0]
    cells = CX * CY * CZ
    owners = lax.axis_size(("gx", "gy"))
    local_pot = potential.reshape(rows_x, rows_y, ZN, 1)
    cell_mask = (pair_cell[0][:, None] == jnp.arange(cells, dtype=jnp.int32)[None, :]).astype(jnp.float32)
    one_hot = (
        slot_atom[0][:, None] == jnp.arange(atoms, dtype=jnp.int32)[None, :]
    ).astype(jnp.float32)
    rows = -(-nproj // 8) * 8
    tile_all = jnp.pad(pair_tile[0], ((0, 0), (0, rows - nproj), (0, 0))).reshape(slots * rows, npc)
    tile_t = tile_all.T
    mask_all = jnp.repeat(cell_mask, rows, axis=0)
    incoming = one_hot.reshape(owners, CAP, atoms)
    hot_k = [incoming[:, k] for k in range(CAP)]
    coupling_pad = jnp.pad(coupling, ((0, 0), (0, rows - nproj), (0, rows - nproj)))

    def exchange(values):
        return lax.all_to_all(values, ("gx", "gy"), split_axis=0, concat_axis=0, tiled=True)

    def owner_work(received):
        atom_sums = None
        for k in range(CAP):
            full = jnp.einsum("sa,spx->apx", hot_k[k], received, precision=PRECISE)
            part = full[:, :, k * W : (k + 1) * W]
            atom_sums = part if atom_sums is None else atom_sums + part
        applied = jnp.einsum("apq,aqw->apw", coupling_pad, atom_sums, precision=PRECISE)
        return jnp.concatenate(
            [jnp.einsum("sa,apw->spw", hot_k[k], applied, precision=PRECISE) for k in range(CAP)],
            axis=-1,
        )

    def apply_operator(current):
        face_x = shifted(current[:1], "gx", -1)
        face_y = shifted(current[:, :1], "gy", -1)
        corner = diagonal(current[:1, :1], -1)
        extended = jnp.concatenate(
            [
                jnp.concatenate([current, face_y], axis=1),
                jnp.concatenate([face_x, corner], axis=1),
            ],
            axis=0,
        )
        cell_in = gather_cells(extended)
        every_cell = jnp.dot(tile_all, cell_in, precision=DENSE)
        picked = None
        for c in range(cells):
            term = every_cell[:, c * W : (c + 1) * W] * mask_all[:, c : c + 1]
            picked = term if picked is None else picked + term
        picked = picked.reshape(owners, CAP, rows, W)
        send = jnp.concatenate([picked[:, k] for k in range(CAP)], axis=-1)
        returned = exchange(owner_work(exchange(send)))
        by_slot = jnp.stack(
            [returned[:, :, k * W : (k + 1) * W] for k in range(CAP)], axis=1
        ).reshape(slots * rows, W)
        spread_in = jnp.concatenate([by_slot * mask_all[:, c : c + 1] for c in range(cells)], axis=1)
        spread = jnp.dot(cell_matrix, cell_in, precision=DENSE) + jnp.dot(
            tile_t, spread_in, precision=DENSE
        )
        summed = scatter_cells(spread, W)
        from_y = shifted(summed[:rows_x, rows_y], "gy", 1)
        from_x = shifted(summed[rows_x, :rows_y], "gx", 1)
        from_corner = diagonal(summed[rows_x, rows_y], 1)
        summed = summed[:rows_x, :rows_y].at[:, 0].add(from_y)
        summed = summed.at[0].add(from_x).at[0, 0].add(from_corner)
        return summed + local_pot * current

    previous = wavefunctions.reshape(rows_x, rows_y, ZN, W)
    for filter_index in range(FILTERS):
        lower_bound = bounds[filter_index, 0]
        low_end = bounds[filter_index, 1]
        high_end = bounds[filter_index, 2]
        half_width = (high_end - low_end) / 2.0
        centre = (high_end + low_end) / 2.0
        sigma_now = half_width / (lower_bound - centre)
        gamma_term = 2.0 / sigma_now
        current = sigma_now / half_width * (apply_operator(previous) - centre * previous)
        sigma_next = 1.0 / (gamma_term - sigma_now)
        following = (
            2.0 * sigma_next / half_width * (apply_operator(current) - centre * current)
            - sigma_now * sigma_next * previous
        )
        current = following
        sigma_now = sigma_next
        previous = current
    return previous.reshape(rows_x, rows_y * ZN * W)


def solution(mesh):
    placed = (
        P("gx", "gy"),
        P("gx", "gy"),
        P(),
        P(("gx", "gy"), None),
        P(("gx", "gy"), None, None, None),
        P(("gx", "gy"), None),
        P(("gx", "gy"), None, None),
        P(),
    )
    return jax.shard_map(body, mesh=mesh, in_specs=placed, out_specs=P("gx", "gy"), check_vma=False)
```

```python
import jax
import jax.numpy as jnp
from jax import lax
from jax.sharding import PartitionSpec as P

DEG = 6
W = 64
CX = 2
CY = 1
CZ = 2
FILTERS = 2
ZN = 12
CAP = 2


PRECISE = lax.Precision.HIGHEST
DENSE = lax.Precision.HIGH


def shifted(value, axis, steps):
    count = lax.axis_size(axis)
    pairs = [(source, (source + steps) % count) for source in range(count)]
    return lax.ppermute(value, axis, pairs)


def diagonal(value, steps):
    count_x = lax.axis_size("gx")
    count_y = lax.axis_size("gy")
    pairs = [
        (u * count_y + v, ((u + steps) % count_x) * count_y + (v + steps) % count_y)
        for u in range(count_x)
        for v in range(count_y)
    ]
    return lax.ppermute(value, ("gx", "gy"), pairs)


def cell_ranges():
    for p in range(CX):
        for q in range(CY):
            for r in range(CZ):
                yield p * DEG, q * DEG, r * DEG


def gather_cells(extended):
    closed = jnp.concatenate([extended, extended[:, :, :1]], axis=2)
    blocks = [
        closed[x0 : x0 + DEG + 1, y0 : y0 + DEG + 1, z0 : z0 + DEG + 1]
        for x0, y0, z0 in cell_ranges()
    ]
    return jnp.concatenate(blocks, axis=-1).reshape((DEG + 1) ** 3, -1)


def scatter_cells(cell_out, columns):
    nx, ny = CX * DEG + 1, CY * DEG + 1
    total = None
    for index, (x0, y0, z0) in enumerate(cell_ranges()):
        block = cell_out[:, index * columns : (index + 1) * columns].reshape(DEG + 1, DEG + 1, DEG + 1, columns)
        spans = ((x0, nx - x0 - DEG - 1), (y0, ny - y0 - DEG - 1))
        if z0 + DEG < ZN:
            pieces = [jnp.pad(block, spans + ((z0, ZN - z0 - DEG - 1), (0, 0)))]
        else:
            pieces = [
                jnp.pad(block[:, :, :DEG], spans + ((z0, ZN - z0 - DEG), (0, 0))),
                jnp.pad(block[:, :, DEG:], spans + ((0, ZN - 1), (0, 0))),
            ]
        for padded in pieces:
            total = padded if total is None else total + padded
    return total


def body(wavefunctions, potential, cell_matrix, pair_cell, pair_tile, slot_atom, coupling, bounds):
    rows_x = wavefunctions.shape[0]
    rows_y = potential.shape[1] // ZN
    slots, nproj, npc = pair_tile.shape[1:]
    atoms = coupling.shape[0]
    cells = CX * CY * CZ
    owners = lax.axis_size(("gx", "gy"))
    local_pot = potential.reshape(rows_x, rows_y, ZN, 1)
    cell_mask = (pair_cell[0][:, None] == jnp.arange(cells, dtype=jnp.int32)[None, :]).astype(jnp.float32)
    one_hot = (
        slot_atom[0][:, None] == jnp.arange(atoms, dtype=jnp.int32)[None, :]
    ).astype(jnp.float32)
    rows = -(-nproj // 8) * 8
    tile_all = jnp.pad(pair_tile[0], ((0, 0), (0, rows - nproj), (0, 0))).reshape(slots * rows, npc)
    tile_t = tile_all.T
    mask_all = jnp.repeat(cell_mask, rows, axis=0)
    incoming = one_hot.reshape(owners, CAP, atoms)
    hot_k = [incoming[:, k] for k in range(CAP)]
    coupling_pad = jnp.pad(coupling, ((0, 0), (0, rows - nproj), (0, rows - nproj)))

    def exchange(values):
        return lax.all_to_all(values, ("gx", "gy"), split_axis=0, concat_axis=0, tiled=True)

    def owner_work(received):
        atom_sums = None
        for k in range(CAP):
            full = jnp.einsum("sa,spx->apx", hot_k[k], received, precision=PRECISE)
            part = full[:, :, k * W : (k + 1) * W]
            atom_sums = part if atom_sums is None else atom_sums + part
        applied = jnp.einsum("apq,aqw->apw", coupling_pad, atom_sums, precision=PRECISE)
        answers = jnp.einsum("ska,apw->spkw", incoming, applied, precision=PRECISE)
        return answers.reshape(owners, rows, CAP * W)

    def apply_operator(current):
        face_x = shifted(current[:1], "gx", -1)
        face_y = shifted(current[:, :1], "gy", -1)
        corner = diagonal(current[:1, :1], -1)
        extended = jnp.concatenate(
            [
                jnp.concatenate([current, face_y], axis=1),
                jnp.concatenate([face_x, corner], axis=1),
            ],
            axis=0,
        )
        cell_in = gather_cells(extended)
        every_cell = jnp.dot(tile_all, cell_in, precision=DENSE)
        picked = None
        for c in range(cells):
            term = every_cell[:, c * W : (c + 1) * W] * mask_all[:, c : c + 1]
            picked = term if picked is None else picked + term
        picked = picked.reshape(owners, CAP, rows, W)
        send = jnp.concatenate([picked[:, k] for k in range(CAP)], axis=-1)
        returned = exchange(owner_work(exchange(send)))
        by_slot = jnp.stack(
            [returned[:, :, k * W : (k + 1) * W] for k in range(CAP)], axis=1
        ).reshape(slots * rows, W)
        spread_in = jnp.concatenate([by_slot * mask_all[:, c : c + 1] for c in range(cells)], axis=1)
        spread = jnp.dot(cell_matrix, cell_in, precision=DENSE) + jnp.dot(
            tile_t, spread_in, precision=DENSE
        )
        summed = scatter_cells(spread, W)
        from_y = shifted(summed[:rows_x, rows_y], "gy", 1)
        from_x = shifted(summed[rows_x, :rows_y], "gx", 1)
        from_corner = diagonal(summed[rows_x, rows_y], 1)
        summed = summed[:rows_x, :rows_y].at[:, 0].add(from_y)
        summed = summed.at[0].add(from_x).at[0, 0].add(from_corner)
        return summed + local_pot * current

    previous = wavefunctions.reshape(rows_x, rows_y, ZN, W)
    for filter_index in range(FILTERS):
        lower_bound = bounds[filter_index, 0]
        low_end = bounds[filter_index, 1]
        high_end = bounds[filter_index, 2]
        half_width = (high_end - low_end) / 2.0
        centre = (high_end + low_end) / 2.0
        sigma_now = half_width / (lower_bound - centre)
        gamma_term = 2.0 / sigma_now
        current = sigma_now / half_width * (apply_operator(previous) - centre * previous)
        sigma_next = 1.0 / (gamma_term - sigma_now)
        following = (
            2.0 * sigma_next / half_width * (apply_operator(current) - centre * current)
            - sigma_now * sigma_next * previous
        )
        current = following
        sigma_now = sigma_next
        previous = current
    return previous.reshape(rows_x, rows_y * ZN * W)


def solution(mesh):
    placed = (
        P("gx", "gy"),
        P("gx", "gy"),
        P(),
        P(("gx", "gy"), None),
        P(("gx", "gy"), None, None, None),
        P(("gx", "gy"), None),
        P(("gx", "gy"), None, None),
        P(),
    )
    return jax.shard_map(body, mesh=mesh, in_specs=placed, out_specs=P("gx", "gy"), check_vma=False)
```
